256 devices in a mesh: blk: 32 (over y, z), band: 8 (over x, core).
Axes of the slice: x: 4, y: 4, z: 8, core: 2. Of those that a mesh axis runs over, the one named last changes fastest.
Arguments:
- solution: float32 [512, 2, 4096], P('blk', None, 'band'), may hold values from -6 to 6
- residual: float32 [512, 2, 4096], P('blk', None, 'band'), may hold values from -4 to 4
- direction: float32 [512, 2, 4096], P('blk', None, 'band'), may hold values from -6 to 6
- prior_inverse: float32 [4096], P('band'), may hold values from 0.3 to 3
- preconditioner: float32 [4096], P('band'), may hold values from 0.2 to 2
- beam_window: float32 [8, 4096], P('band'), may hold values from 0.3 to 1
- legendre: bfloat16 [512, 64, 4096], P('blk'), may hold values from -4 to 4, as said below
- mode_orders: int32 [512], replicated, may hold values from 0 to 4095, as said below
- noise_weight: float32 [8, 64, 8192], P('band', 'blk'), may hold values from 0.2 to 2
- smoother_blocks: float32 [32, 64, 64], replicated, may hold values from -0.5 to 0.6
- tile_slots: int32 [4096], P('blk'), may hold values from 0 to 255, as said below
- tile_kinds: int32 [4096], P('blk'), may hold values from 0 to 31
Outputs:
- solution_next: float32 [512, 2, 4096], P('blk', None, 'band')
- residual_next: float32 [512, 2, 4096], P('blk', None, 'band')
- direction_next: float32 [512, 2, 4096], P('blk', None, 'band')
The draws below stay inside these ranges and needn't reach their ends.
Inputs may be any that keep to these rules, and one draw needn't show every extreme that they name: `mode_orders`: 512 distinct orders, among them every order below the larger of 1 and 32. `legendre`: zero wherever the multipole l is below the slot's order in mode_orders. `tile_slots`: within the 128 entries of one cycle group, distinct tile numbers of that group's 2 * 128 tiles.
All inputs are finite; a program needn't handle non-finite values.
Results may differ from the reference program's by a relative error of at most 0.0016.
Values may be sent and summed in bfloat16 or wider, within the bound.
No kernel may reach another device: no remote copies, remote signals or barrier semaphores. Data moves between devices by JAX's collectives and lax.ppermute only.
A program may use at most 128 MiB of HBM per device.

```python
import math
import jax
import jax.numpy as jnp
from jax import lax

L = 4096
NPHI = 8192
TILE = 64
NTYPES = 32
R_DEV = 2
TILES_DEV = 128
M = 512
R = 64
TILES = 4096
NBAND = 8


def order_helper(key):
    base_key = jax.random.fold_in(key, 11)
    low_count = max(1, M // 16)
    low_orders = jnp.arange(low_count, dtype=jnp.int32)
    remainder = jax.random.permutation(jax.random.fold_in(base_key, 1), L - 1 - low_count)[:M - low_count - 1] + low_count
    values = jnp.concatenate([jnp.array([L - 1], jnp.int32), low_orders, remainder.astype(jnp.int32)])
    shuffle = jax.random.permutation(jax.random.fold_in(base_key, 2), M)
    return values[shuffle]


def state_helper(key):
    base_key = jax.random.fold_in(key, 41)
    log_span = math.log(10.0)
    resid = jax.random.truncated_normal(jax.random.fold_in(base_key, 1), -4.0, 4.0, (M, 2, L), jnp.float32)
    extra = jax.random.truncated_normal(jax.random.fold_in(base_key, 3), -4.0, 4.0, (M, 2, L), jnp.float32)
    precond = 0.2 * jnp.exp(jax.random.uniform(jax.random.fold_in(base_key, 2), (L,), jnp.float32, 0.0, log_span))
    searched = jnp.clip(precond[None, None, :] * resid + 0.3 * extra, -6.0, 6.0)
    return (resid, precond, searched)


def draw_residual(key, part):
    return state_helper(key)[0]


def draw_preconditioner(key, part):
    return state_helper(key)[1]


def draw_direction(key, part):
    return state_helper(key)[2]


def draw_smoother_blocks(key, part):
    value_key = jax.random.fold_in(key, 31)
    values = 0.05 + 0.125 * jax.random.truncated_normal(value_key, -4.0, 4.0, (NTYPES, TILE, TILE), jnp.float32)
    return values


def draw_mode_orders(key, part):
    return order_helper(key)


def draw_legendre(key, part):
    orders = order_helper(key)
    value_key = jax.random.fold_in(key, 3)
    values = jax.random.truncated_normal(value_key, -4.0, 4.0, (M, R, L), jnp.float32)
    degrees = jnp.arange(L, dtype=jnp.int32)
    live_mask = (degrees[None, None, :] >= orders[:, None, None]).astype(jnp.float32)
    spans = (L - orders).astype(jnp.float32)
    return (values * live_mask / jnp.sqrt(spans)[:, None, None]).astype(jnp.bfloat16)


def draw_tile_slots(key, part):
    tile_total = R_DEV * NPHI // TILE
    groups = TILES // TILES_DEV

    def one_group(group_index):
        group_key = jax.random.fold_in(key, group_index)
        remainder = jax.random.permutation(jax.random.fold_in(group_key, 1), tile_total - 2)[:TILES_DEV - 2] + 1
        values = jnp.concatenate([jnp.array([tile_total - 1, 0], jnp.int32), remainder.astype(jnp.int32)])
        return values[jax.random.permutation(jax.random.fold_in(group_key, 2), TILES_DEV)]
    return jax.vmap(one_group)(jnp.arange(groups, dtype=jnp.int32)).reshape(TILES)


def with_ends(entries, key, low, largest):
    place = [jax.random.randint(jax.random.fold_in(key, axis), (), 0, length) for axis, length in enumerate(entries.shape)]
    widest = entries.shape.index(max(entries.shape))
    next_to = place[:widest] + [(place[widest] + 1) % entries.shape[widest]] + place[widest + 1:]
    return entries.at[tuple(place)].set(low).at[tuple(next_to)].set(largest)


def levels(stream_key, dims, shards, least, top_value):
    factor_of, own = 1.0, jax.random.fold_in(stream_key, 6)
    for axis_at, parts in shards:
        steps = jnp.exp(jax.random.uniform(jax.random.fold_in(own, axis_at), (parts,), jnp.float32, least / len(shards), top_value / len(shards)))
        factor_of = factor_of * jnp.repeat(steps, dims[axis_at] // parts).reshape([-1 if axis == axis_at else 1 for axis in range(len(dims))])
    return factor_of


def scatter_about(key, extent, width, bound, pieces=(), kind=jnp.bfloat16):
    factor_of = levels(key, extent, pieces, -0.22, 0.18) if pieces else 1.0
    drawn = jax.random.normal(key, extent, jnp.float32) * width * factor_of
    return jnp.minimum(jnp.maximum(drawn, -bound), bound).astype(kind)


def setup_inputs(seed: int = 0) -> dict:
    arg_keys = jax.random.split(jax.random.key(seed), 13)
    solution = scatter_about(arg_keys[0], (M, 2, L), 1.0, 6.0, ((0, 32), (2, 8)), jnp.float32)
    residual = draw_residual(jax.random.fold_in(arg_keys[12], 71), 0)
    direction = draw_direction(jax.random.fold_in(arg_keys[12], 71), 0)
    prior_inverse = jnp.clip(jnp.exp(math.log(3.0) - 2.3025851 * jax.random.uniform(arg_keys[3], (L,), jnp.float32) ** levels(arg_keys[3], (L,), ((0, 8),), -0.2, 0.2)), 0.3, 3.0)
    preconditioner = draw_preconditioner(jax.random.fold_in(arg_keys[12], 71), 0)
    beam_window = jnp.clip(jnp.exp(math.log(1.0) - 1.2039728 * jax.random.uniform(arg_keys[5], (NBAND, L), jnp.float32) ** levels(arg_keys[5], (NBAND, L), ((0, 8),), -0.2, 0.2)), 0.3, 1.0)
    legendre = draw_legendre(jax.random.fold_in(arg_keys[12], 71), 0)
    mode_orders = draw_mode_orders(jax.random.fold_in(arg_keys[12], 71), 0)
    noise_weight = jnp.clip(jnp.exp(math.log(2.0) - 2.3025851 * jax.random.uniform(arg_keys[8], (NBAND, R, NPHI), jnp.float32) ** levels(arg_keys[8], (NBAND, R, NPHI), ((0, 8), (1, 32)), -0.2, 0.2)), 0.2, 2.0)
    smoother_blocks = draw_smoother_blocks(jax.random.fold_in(arg_keys[12], 71), 0)
    tile_slots = draw_tile_slots(jax.random.fold_in(arg_keys[12], 71), 0)
    tile_kinds = with_ends(jax.random.randint(arg_keys[11], (TILES,), 0, NTYPES), jax.random.fold_in(arg_keys[11], 1), 0, NTYPES - 1).astype(jnp.int32)
    return {"solution": solution, "residual": residual, "direction": direction, "prior_inverse": prior_inverse, "preconditioner": preconditioner, "beam_window": beam_window, "legendre": legendre, "mode_orders": mode_orders, "noise_weight": noise_weight, "smoother_blocks": smoother_blocks, "tile_slots": tile_slots, "tile_kinds": tile_kinds}


precise = lax.Precision.HIGHEST

def fourier(mode_orders):
    columns = jnp.arange(NPHI, dtype=jnp.int32)
    turn_counts = mode_orders[:, None] * columns[None, :] % NPHI
    angles = turn_counts.astype(jnp.float32) * (2.0 * math.pi / NPHI)
    return (jnp.cos(angles), jnp.sin(angles))

def smooth(pixels, smoother_blocks, tile_slots, tile_kinds):
    tile_rows = pixels.reshape(-1, TILE)
    picked = tile_rows[tile_slots]
    matrices = smoother_blocks[tile_kinds]
    inner_part = jnp.einsum('tij,tj->ti', matrices, picked, precision=precise)
    outer_part = jnp.einsum('tji,tj->ti', matrices, inner_part, precision=precise)
    return jnp.zeros_like(tile_rows).at[tile_slots].add(outer_part).reshape(pixels.shape)

def synth_one(operands):
    return jnp.dot(operands[0], operands[1].T, preferred_element_type=jnp.float32)

def analyse_one(operands):
    return jnp.dot(operands[0], operands[1], preferred_element_type=jnp.float32)

def reference(solution, residual, direction, prior_inverse, preconditioner, beam_window, legendre, mode_orders, noise_weight, smoother_blocks, tile_slots, tile_kinds):
    cosines, sines = fourier(mode_orders)
    norm_scale = 1.0 / math.sqrt(M)
    groups = jnp.arange(TILES, dtype=jnp.int32) // TILES_DEV
    global_slots = (tile_slots + groups * (R_DEV * NPHI // TILE)).astype(jnp.int32)
    summed = jnp.zeros(direction.shape, jnp.float32)
    for band_index in range(NBAND):
        weighted_dir = (beam_window[band_index][None, None, :] * direction).astype(jnp.bfloat16)
        coefficients = lax.map(synth_one, (weighted_dir, legendre))
        pixels = norm_scale * (jnp.einsum('mr,mj->rj', coefficients[:, 0], cosines, precision=precise) - jnp.einsum('mr,mj->rj', coefficients[:, 1], sines, precision=precise))
        noisy = noise_weight[band_index] * pixels + smooth(pixels, smoother_blocks, global_slots, tile_kinds)
        real_terms = norm_scale * jnp.einsum('rj,mj->mr', noisy, cosines, precision=precise)
        imag_terms = -norm_scale * jnp.einsum('rj,mj->mr', noisy, sines, precision=precise)
        cycle_terms = jnp.stack([real_terms, imag_terms], axis=1).astype(jnp.bfloat16)
        harmonic = lax.map(analyse_one, (cycle_terms, legendre))
        summed = summed + beam_window[band_index][None, None, :] * harmonic
    image = prior_inverse[None, None, :] * direction + summed
    scaled_res = preconditioner[None, None, :] * residual
    norm_now = jnp.sum(residual * scaled_res)
    step_size = norm_now / jnp.sum(direction * image)
    solution_next = solution + step_size * direction
    residual_next = residual - step_size * image
    precond_next = preconditioner[None, None, :] * residual_next
    norm_next = jnp.sum(residual_next * precond_next)
    direction_next = precond_next + norm_next / norm_now * direction
    return (solution_next, residual_next, direction_next)
```

```python
import math

import jax
import jax.numpy as jnp
from jax import lax
from jax.sharding import PartitionSpec as P

NPHI = 8192
TILE = 64


precise = lax.Precision.HIGHEST
EVERY = ("blk", "band")


def phases(mode_orders, column_count, stride):
    columns = jnp.arange(column_count, dtype=jnp.int32) * stride
    turn_counts = mode_orders[:, None] * columns[None, :] % NPHI
    angles = turn_counts.astype(jnp.float32) * (2.0 * math.pi / NPHI)
    return (jnp.cos(angles), jnp.sin(angles))


def pick_kind(per_kind, tile_kinds):
    kinds = jnp.arange(per_kind.shape[1], dtype=jnp.int32)
    chosen = tile_kinds[:, None, None] == kinds[None, :, None]
    return jnp.sum(jnp.where(chosen, per_kind, 0.0), axis=1)


def smooth(pixels, smoother_blocks, tile_slots, tile_kinds):
    tile_rows = pixels.reshape(-1, TILE)
    picked = tile_rows[tile_slots]
    inner_all = jnp.einsum("kij,tj->tki", smoother_blocks, picked, precision=precise)
    inner_part = pick_kind(inner_all, tile_kinds)
    outer_all = jnp.einsum("kji,tj->tki", smoother_blocks, inner_part, precision=precise)
    outer_part = pick_kind(outer_all, tile_kinds)
    return jnp.zeros_like(tile_rows).at[tile_slots].add(outer_part).reshape(pixels.shape)


def per_device(
    solution,
    residual,
    direction,
    prior_inverse,
    preconditioner,
    beam_window,
    legendre,
    mode_orders,
    noise_weight,
    smoother_blocks,
    tile_slots,
    tile_kinds,
):
    nblk = lax.axis_size("blk")
    nband = lax.axis_size("band")
    band = lax.axis_index("band")
    orders_dev, parts, width = direction.shape
    cycles_all = legendre.shape[1]
    cycles_dev = cycles_all // nblk
    order_count = mode_orders.shape[0]
    norm_scale = 1.0 / math.sqrt(order_count)

    beam_here = lax.all_to_all(
        beam_window.reshape(nband, width), "band", split_axis=0, concat_axis=0, tiled=True
    )
    legendre_here = lax.dynamic_slice_in_dim(legendre, band * width, width, 2)

    weighted = (beam_here[None, :, None, :] * direction[:, None, :, :]).astype(jnp.bfloat16)
    weighted = weighted.reshape(orders_dev, nband * parts, width)
    partial = jnp.einsum(
        "sql,srl->sqr", weighted, legendre_here, preferred_element_type=jnp.float32
    )
    partial = partial.reshape(orders_dev, nband, parts, nblk, cycles_dev)
    outgoing = partial.transpose(3, 1, 0, 2, 4).reshape(
        nblk * nband, orders_dev, parts, cycles_dev
    )
    incoming = lax.all_to_all(outgoing, EVERY, split_axis=0, concat_axis=0, tiled=True)
    cycle_coefficients = jnp.sum(
        incoming.reshape(nblk, nband, orders_dev, parts, cycles_dev), axis=1
    ).reshape(order_count, parts, cycles_dev)

    cycle_count = cycles_dev
    outer_cos, outer_sin = phases(mode_orders, NPHI // 128, 128)
    inner_cos, inner_sin = phases(mode_orders, 128, 1)
    real_part = cycle_coefficients[:, 0, :, None]
    imag_part = cycle_coefficients[:, 1, :, None]
    upper_part = real_part * outer_cos[:, None, :] - imag_part * outer_sin[:, None, :]
    lower_part = real_part * outer_sin[:, None, :] + imag_part * outer_cos[:, None, :]
    pixel_grid = jnp.einsum("mra,mb->rab", upper_part, inner_cos, precision=precise) - jnp.einsum(
        "mra,mb->rab", lower_part, inner_sin, precision=precise
    )
    pixels = norm_scale * pixel_grid.reshape(cycle_count, NPHI)
    noisy = noise_weight[0] * pixels + smooth(pixels, smoother_blocks, tile_slots, tile_kinds)
    noisy_grid = noisy.reshape(cycle_count, NPHI // 128, 128)
    cos_sums = jnp.einsum("rab,mb->mra", noisy_grid, inner_cos, precision=precise)
    sin_sums = jnp.einsum("rab,mb->mra", noisy_grid, inner_sin, precision=precise)
    real_terms = norm_scale * (
        jnp.einsum("mra,ma->mr", cos_sums, outer_cos, precision=precise)
        - jnp.einsum("mra,ma->mr", sin_sums, outer_sin, precision=precise)
    )
    imag_terms = -norm_scale * (
        jnp.einsum("mra,ma->mr", cos_sums, outer_sin, precision=precise)
        + jnp.einsum("mra,ma->mr", sin_sums, outer_cos, precision=precise)
    )
    cycle_terms = jnp.stack([real_terms, imag_terms], axis=1).astype(jnp.bfloat16)

    per_owner = cycle_terms.reshape(nblk, 1, orders_dev, parts, cycles_dev)
    returning = jnp.broadcast_to(
        per_owner, (nblk, nband, orders_dev, parts, cycles_dev)
    ).reshape(nblk * nband, orders_dev, parts, cycles_dev)
    arrived = lax.all_to_all(returning, EVERY, split_axis=0, concat_axis=0, tiled=True)
    mode_terms = arrived.reshape(nblk, nband, orders_dev, parts, cycles_dev)
    mode_terms = mode_terms.transpose(2, 1, 3, 0, 4).reshape(orders_dev, nband * parts, cycles_all)
    harmonic = jnp.einsum(
        "sqr,srl->sql", mode_terms, legendre_here, preferred_element_type=jnp.float32
    ).reshape(orders_dev, nband, parts, width)
    summed = jnp.sum(beam_here[None, :, None, :] * harmonic, axis=1)

    image = prior_inverse[None, None, :] * direction + summed
    scaled_res = preconditioner[None, None, :] * residual
    scaled_image = preconditioner[None, None, :] * image
    local_sums = jnp.stack(
        [
            jnp.sum(residual * scaled_res),
            jnp.sum(direction * image),
            jnp.sum(scaled_res * image),
            jnp.sum(scaled_image * image),
        ]
    )
    totals = lax.psum(local_sums, EVERY)
    norm_now = totals[0]
    step_size = norm_now / totals[1]
    norm_next = norm_now - step_size * (2.0 * totals[2] - step_size * totals[3])
    residual_next = residual - step_size * image
    precond_next = preconditioner[None, None, :] * residual_next
    solution_next = solution + step_size * direction
    direction_next = precond_next + norm_next / norm_now * direction
    return (solution_next, residual_next, direction_next)


def solution(mesh):
    return jax.shard_map(
        per_device,
        mesh=mesh,
        in_specs=(
            P("blk", None, "band"),
            P("blk", None, "band"),
            P("blk", None, "band"),
            P("band"),
            P("band"),
            P("band", None),
            P("blk", None, None),
            P(),
            P("band", "blk", None),
            P(),
            P("blk"),
            P("blk"),
        ),
        out_specs=(P("blk", None, "band"), P("blk", None, "band"), P("blk", None, "band")),
        check_vma=False,
    )
```

```python
import math

import jax
import jax.numpy as jnp
from jax import lax
from jax.sharding import PartitionSpec as P

NPHI = 8192
TILE = 64


precise = lax.Precision.HIGHEST
EVERY = ("blk", "band")


def phases(mode_orders, column_count, stride):
    columns = jnp.arange(column_count, dtype=jnp.int32) * stride
    turn_counts = mode_orders[:, None] * columns[None, :] % NPHI
    angles = turn_counts.astype(jnp.float32) * (2.0 * math.pi / NPHI)
    return (jnp.cos(angles), jnp.sin(angles))


def pick_kind(per_kind, tile_kinds):
    kinds = jnp.arange(per_kind.shape[1], dtype=jnp.int32)
    chosen = tile_kinds[:, None, None] == kinds[None, :, None]
    return jnp.sum(jnp.where(chosen, per_kind, 0.0), axis=1)


def smooth(pixels, smoother_blocks, tile_slots, tile_kinds):
    tile_rows = pixels.reshape(-1, TILE)
    picked = tile_rows[tile_slots]
    inner_all = jnp.einsum("kij,tj->tki", smoother_blocks, picked, precision=precise)
    inner_part = pick_kind(inner_all, tile_kinds)
    outer_all = jnp.einsum("kji,tj->tki", smoother_blocks, inner_part, precision=precise)
    outer_part = pick_kind(outer_all, tile_kinds)
    return jnp.zeros_like(tile_rows).at[tile_slots].add(outer_part).reshape(pixels.shape)


def per_device(
    solution,
    residual,
    direction,
    prior_inverse,
    preconditioner,
    beam_window,
    legendre,
    mode_orders,
    noise_weight,
    smoother_blocks,
    tile_slots,
    tile_kinds,
):
    nblk = lax.axis_size("blk")
    nband = lax.axis_size("band")
    band = lax.axis_index("band")
    orders_dev, parts, width = direction.shape
    cycles_all = legendre.shape[1]
    cycles_dev = cycles_all // nblk
    order_count = mode_orders.shape[0]
    norm_scale = 1.0 / math.sqrt(order_count)

    beam_here = lax.all_to_all(
        beam_window.reshape(nband, width), "band", split_axis=0, concat_axis=0, tiled=True
    )
    legendre_here = lax.dynamic_slice_in_dim(legendre, band * width, width, 2)

    weighted = (beam_here[None, :, None, :] * direction[:, None, :, :]).astype(jnp.bfloat16)
    weighted = weighted.reshape(orders_dev, nband * parts, width)
    partial = jnp.einsum(
        "sql,srl->sqr", weighted, legendre_here, preferred_element_type=jnp.float32
    )
    partial = partial.reshape(orders_dev, nband, parts, nblk, cycles_dev)
    outgoing = partial.transpose(3, 1, 0, 2, 4).reshape(
        nblk * nband, orders_dev, parts, cycles_dev
    )
    incoming = lax.all_to_all(outgoing, EVERY, split_axis=0, concat_axis=0, tiled=True)
    cycle_coefficients = jnp.sum(
        incoming.reshape(nblk, nband, orders_dev, parts, cycles_dev), axis=1
    ).reshape(order_count, parts, cycles_dev)

    cycle_count = cycles_dev
    outer_cos, outer_sin = phases(mode_orders, NPHI // 128, 128)
    inner_cos, inner_sin = phases(mode_orders, 128, 1)
    real_part = cycle_coefficients[:, 0, :, None]
    imag_part = cycle_coefficients[:, 1, :, None]
    upper_part = real_part * outer_cos[:, None, :] - imag_part * outer_sin[:, None, :]
    lower_part = real_part * outer_sin[:, None, :] + imag_part * outer_cos[:, None, :]
    pixel_grid = jnp.einsum("mra,mb->rab", upper_part, inner_cos, precision=precise) - jnp.einsum(
        "mra,mb->rab", lower_part, inner_sin, precision=precise
    )
    pixels = norm_scale * pixel_grid.reshape(cycle_count, NPHI)
    noisy = noise_weight[0] * pixels + smooth(pixels, smoother_blocks, tile_slots, tile_kinds)
    noisy_grid = noisy.reshape(cycle_count, NPHI // 128, 128)
    cos_sums = jnp.einsum("rab,mb->mra", noisy_grid, inner_cos, precision=precise)
    sin_sums = jnp.einsum("rab,mb->mra", noisy_grid, inner_sin, precision=precise)
    real_terms = norm_scale * (
        jnp.einsum("mra,ma->mr", cos_sums, outer_cos, precision=precise)
        - jnp.einsum("mra,ma->mr", sin_sums, outer_sin, precision=precise)
    )
    imag_terms = -norm_scale * (
        jnp.einsum("mra,ma->mr", cos_sums, outer_sin, precision=precise)
        + jnp.einsum("mra,ma->mr", sin_sums, outer_cos, precision=precise)
    )
    cycle_terms = jnp.stack([real_terms, imag_terms], axis=1).astype(jnp.bfloat16)

    per_owner = cycle_terms.reshape(nblk, 1, orders_dev, parts, cycles_dev)
    returning = jnp.broadcast_to(
        per_owner, (nblk, nband, orders_dev, parts, cycles_dev)
    ).reshape(nblk * nband, orders_dev, parts, cycles_dev)
    arrived = lax.all_to_all(returning, EVERY, split_axis=0, concat_axis=0, tiled=True)
    mode_terms = arrived.reshape(nblk, nband, orders_dev, parts, cycles_dev)
    mode_terms = mode_terms.transpose(2, 1, 3, 0, 4).reshape(orders_dev, nband * parts, cycles_all)
    harmonic = jnp.einsum(
        "sqr,srl->sql", mode_terms, legendre_here, preferred_element_type=jnp.float32
    ).reshape(orders_dev, nband, parts, width)
    summed = jnp.sum(beam_here[None, :, None, :] * harmonic, axis=1)

    image = prior_inverse[None, None, :] * direction + summed
    scaled_res = preconditioner[None, None, :] * residual
    scaled_image = preconditioner[None, None, :] * image
    local_sums = jnp.stack(
        [
            jnp.sum(residual * scaled_res),
            jnp.sum(direction * image),
            jnp.sum(scaled_res * image),
            jnp.sum(scaled_image * image),
        ]
    )
    shared = jnp.broadcast_to(local_sums[None], (nblk * nband, local_sums.shape[0]))
    totals = jnp.sum(lax.all_to_all(shared, EVERY, split_axis=0, concat_axis=0, tiled=True), axis=0)
    norm_now = totals[0]
    step_size = norm_now / totals[1]
    norm_next = norm_now - step_size * (2.0 * totals[2] - step_size * totals[3])
    residual_next = residual - step_size * image
    precond_next = preconditioner[None, None, :] * residual_next
    solution_next = solution + step_size * direction
    direction_next = precond_next + norm_next / norm_now * direction
    return (solution_next, residual_next, direction_next)


def solution(mesh):
    return jax.shard_map(
        per_device,
        mesh=mesh,
        in_specs=(
            P("blk", None, "band"),
            P("blk", None, "band"),
            P("blk", None, "band"),
            P("band"),
            P("band"),
            P("band", None),
            P("blk", None, None),
            P(),
            P("band", "blk", None),
            P(),
            P("blk"),
            P("blk"),
        ),
        out_specs=(P("blk", None, "band"), P("blk", None, "band"), P("blk", None, "band")),
        check_vma=False,
    )
```

```python
import math

import jax
import jax.numpy as jnp
from jax import lax
from jax.sharding import PartitionSpec as P

NPHI = 8192
TILE = 64


precise = lax.Precision.HIGHEST
EVERY = ("blk", "band")


def phases(mode_orders, column_count, stride):
    columns = jnp.arange(column_count, dtype=jnp.int32) * stride
    turn_counts = mode_orders[:, None] * columns[None, :] % NPHI
    angles = turn_counts.astype(jnp.float32) * (2.0 * math.pi / NPHI)
    return (jnp.cos(angles), jnp.sin(angles))


def pick_kind(per_kind, tile_kinds):
    kinds = jnp.arange(per_kind.shape[1], dtype=jnp.int32)
    chosen = tile_kinds[:, None, None] == kinds[None, :, None]
    return jnp.sum(jnp.where(chosen, per_kind, 0.0), axis=1)


def smooth(pixels, smoother_blocks, tile_slots, tile_kinds):
    tile_rows = pixels.reshape(-1, TILE)
    picked = tile_rows[tile_slots]
    inner_all = jnp.einsum("kij,tj->tki", smoother_blocks, picked, precision=precise)
    inner_part = pick_kind(inner_all, tile_kinds)
    outer_all = jnp.einsum("kji,tj->tki", smoother_blocks, inner_part, precision=precise)
    outer_part = pick_kind(outer_all, tile_kinds)
    return jnp.zeros_like(tile_rows).at[tile_slots].add(outer_part).reshape(pixels.shape)


def per_device(
    solution,
    residual,
    direction,
    prior_inverse,
    preconditioner,
    beam_window,
    legendre,
    mode_orders,
    noise_weight,
    smoother_blocks,
    tile_slots,
    tile_kinds,
):
    nblk = lax.axis_size("blk")
    nband = lax.axis_size("band")
    band = lax.axis_index("band")
    orders_dev, parts, width = direction.shape
    cycles_all = legendre.shape[1]
    cycles_dev = cycles_all // nblk
    order_count = mode_orders.shape[0]
    norm_scale = 1.0 / math.sqrt(order_count)

    beam_here = lax.all_to_all(
        beam_window.reshape(nband, width), "band", split_axis=0, concat_axis=0, tiled=True
    )
    legendre_here = lax.dynamic_slice_in_dim(legendre, band * width, width, 2)

    weighted = (beam_here[None, :, None, :] * direction[:, None, :, :]).astype(jnp.bfloat16)
    weighted = weighted.reshape(orders_dev, nband * parts, width)
    partial = jnp.einsum(
        "sql,srl->sqr", weighted, legendre_here, preferred_element_type=jnp.float32
    )
    partial = partial.reshape(orders_dev, nband, parts, nblk, cycles_dev)
    chunk = orders_dev * parts * cycles_dev
    outgoing = partial.transpose(3, 1, 0, 2, 4).reshape(nblk * nband, chunk)
    incoming = lax.all_to_all(outgoing, EVERY, split_axis=0, concat_axis=0, tiled=True)
    cycle_coefficients = jnp.sum(
        incoming.reshape(nblk, nband, orders_dev, parts, cycles_dev), axis=1
    ).reshape(order_count, parts, cycles_dev)

    cycle_count = cycles_dev
    outer_cos, outer_sin = phases(mode_orders, NPHI // 128, 128)
    inner_cos, inner_sin = phases(mode_orders, 128, 1)
    real_part = cycle_coefficients[:, 0, :, None]
    imag_part = cycle_coefficients[:, 1, :, None]
    upper_part = real_part * outer_cos[:, None, :] - imag_part * outer_sin[:, None, :]
    lower_part = real_part * outer_sin[:, None, :] + imag_part * outer_cos[:, None, :]
    pixel_grid = jnp.einsum("mra,mb->rab", upper_part, inner_cos, precision=precise) - jnp.einsum(
        "mra,mb->rab", lower_part, inner_sin, precision=precise
    )
    pixels = norm_scale * pixel_grid.reshape(cycle_count, NPHI)
    noisy = noise_weight[0] * pixels + smooth(pixels, smoother_blocks, tile_slots, tile_kinds)
    noisy_grid = noisy.reshape(cycle_count, NPHI // 128, 128)
    cos_sums = jnp.einsum("rab,mb->mra", noisy_grid, inner_cos, precision=precise)
    sin_sums = jnp.einsum("rab,mb->mra", noisy_grid, inner_sin, precision=precise)
    real_terms = norm_scale * (
        jnp.einsum("mra,ma->mr", cos_sums, outer_cos, precision=precise)
        - jnp.einsum("mra,ma->mr", sin_sums, outer_sin, precision=precise)
    )
    imag_terms = -norm_scale * (
        jnp.einsum("mra,ma->mr", cos_sums, outer_sin, precision=precise)
        + jnp.einsum("mra,ma->mr", sin_sums, outer_cos, precision=precise)
    )
    cycle_terms = jnp.stack([real_terms, imag_terms], axis=1).astype(jnp.bfloat16)

    per_owner = cycle_terms.reshape(nblk, 1, chunk)
    returning = jnp.broadcast_to(per_owner, (nblk, nband, chunk)).reshape(nblk * nband, chunk)
    arrived = lax.all_to_all(returning, EVERY, split_axis=0, concat_axis=0, tiled=True)
    mode_terms = arrived.reshape(nblk, nband, orders_dev, parts, cycles_dev)
    mode_terms = mode_terms.transpose(2, 1, 3, 0, 4).reshape(orders_dev, nband * parts, cycles_all)
    harmonic = jnp.einsum(
        "sqr,srl->sql", mode_terms, legendre_here, preferred_element_type=jnp.float32
    ).reshape(orders_dev, nband, parts, width)
    summed = jnp.sum(beam_here[None, :, None, :] * harmonic, axis=1)

    image = prior_inverse[None, None, :] * direction + summed
    scaled_res = preconditioner[None, None, :] * residual
    scaled_image = preconditioner[None, None, :] * image
    local_sums = jnp.stack(
        [
            jnp.sum(residual * scaled_res),
            jnp.sum(direction * image),
            jnp.sum(scaled_res * image),
            jnp.sum(scaled_image * image),
        ]
    )
    shared = jnp.broadcast_to(local_sums[None], (nblk * nband, local_sums.shape[0]))
    totals = jnp.sum(lax.all_to_all(shared, EVERY, split_axis=0, concat_axis=0, tiled=True), axis=0)
    norm_now = totals[0]
    step_size = norm_now / totals[1]
    norm_next = norm_now - step_size * (2.0 * totals[2] - step_size * totals[3])
    residual_next = residual - step_size * image
    precond_next = preconditioner[None, None, :] * residual_next
    solution_next = solution + step_size * direction
    direction_next = precond_next + norm_next / norm_now * direction
    return (solution_next, residual_next, direction_next)


def solution(mesh):
    return jax.shard_map(
        per_device,
        mesh=mesh,
        in_specs=(
            P("blk", None, "band"),
            P("blk", None, "band"),
            P("blk", None, "band"),
            P("band"),
            P("band"),
            P("band", None),
            P("blk", None, None),
            P(),
            P("band", "blk", None),
            P(),
            P("blk"),
            P("blk"),
        ),
        out_specs=(P("blk", None, "band"), P("blk", None, "band"), P("blk", None, "band")),
        check_vma=False,
    )
```

```python
import math

import jax
import jax.numpy as jnp
from jax import lax
from jax.sharding import PartitionSpec as P

NPHI = 8192
TILE = 64


precise = lax.Precision.HIGHEST
EVERY = ("blk", "band")


def phases(mode_orders, column_count, stride):
    columns = jnp.arange(column_count, dtype=jnp.int32) * stride
    turn_counts = mode_orders[:, None] * columns[None, :] % NPHI
    angles = turn_counts.astype(jnp.float32) * (2.0 * math.pi / NPHI)
    return (jnp.cos(angles), jnp.sin(angles))


def pick_kind(per_kind, tile_kinds):
    kinds = jnp.arange(per_kind.shape[1], dtype=jnp.int32)
    chosen = tile_kinds[:, None, None] == kinds[None, :, None]
    return jnp.sum(jnp.where(chosen, per_kind, 0.0), axis=1)


def smooth(pixels, smoother_blocks, tile_slots, tile_kinds):
    tile_rows = pixels.reshape(-1, TILE)
    picked = tile_rows[tile_slots]
    inner_all = jnp.einsum("kij,tj->tki", smoother_blocks, picked, precision=precise)
    inner_part = pick_kind(inner_all, tile_kinds)
    outer_all = jnp.einsum("kji,tj->tki", smoother_blocks, inner_part, precision=precise)
    outer_part = pick_kind(outer_all, tile_kinds)
    return jnp.zeros_like(tile_rows).at[tile_slots].add(outer_part).reshape(pixels.shape)


def per_device(
    solution,
    residual,
    direction,
    prior_inverse,
    preconditioner,
    beam_window,
    legendre,
    mode_orders,
    noise_weight,
    smoother_blocks,
    tile_slots,
    tile_kinds,
):
    nblk = lax.axis_size("blk")
    nband = lax.axis_size("band")
    band = lax.axis_index("band")
    orders_dev, parts, width = direction.shape
    cycles_all = legendre.shape[1]
    cycles_dev = cycles_all // nblk
    order_count = mode_orders.shape[0]
    norm_scale = 1.0 / math.sqrt(order_count)

    beam_here = lax.all_to_all(
        beam_window.reshape(nband, width), "band", split_axis=0, concat_axis=0, tiled=True
    )
    legendre_here = lax.dynamic_slice_in_dim(legendre, band * width, width, 2)

    weighted = (beam_here[None, :, None, :] * direction[:, None, :, :]).astype(jnp.bfloat16)
    weighted = weighted.reshape(orders_dev, nband * parts, width)
    partial = jnp.einsum(
        "sql,srl->sqr", weighted, legendre_here, preferred_element_type=jnp.float32
    )
    partial = partial.reshape(orders_dev, nband, parts, nblk, cycles_dev)
    chunk = orders_dev * parts * cycles_dev
    outgoing = partial.transpose(3, 1, 0, 2, 4).reshape(nblk * nband, chunk)
    incoming = lax.all_to_all(outgoing, EVERY, split_axis=0, concat_axis=0, tiled=True)
    cycle_coefficients = jnp.sum(
        incoming.reshape(nblk, nband, orders_dev, parts, cycles_dev), axis=1
    ).reshape(order_count, parts, cycles_dev)

    cycle_count = cycles_dev
    outer_cos, outer_sin = phases(mode_orders, NPHI // 128, 128)
    inner_cos, inner_sin = phases(mode_orders, 128, 1)
    real_part = cycle_coefficients[:, 0, :, None]
    imag_part = cycle_coefficients[:, 1, :, None]
    upper_part = real_part * outer_cos[:, None, :] - imag_part * outer_sin[:, None, :]
    lower_part = real_part * outer_sin[:, None, :] + imag_part * outer_cos[:, None, :]
    pixel_grid = jnp.einsum("mra,mb->rab", upper_part, inner_cos, precision=precise) - jnp.einsum(
        "mra,mb->rab", lower_part, inner_sin, precision=precise
    )
    pixels = norm_scale * pixel_grid.reshape(cycle_count, NPHI)
    noisy = noise_weight[0] * pixels + smooth(pixels, smoother_blocks, tile_slots, tile_kinds)
    noisy_grid = noisy.reshape(cycle_count, NPHI // 128, 128)
    cos_sums = jnp.einsum("rab,mb->mra", noisy_grid, inner_cos, precision=precise)
    sin_sums = jnp.einsum("rab,mb->mra", noisy_grid, inner_sin, precision=precise)
    real_terms = norm_scale * (
        jnp.einsum("mra,ma->mr", cos_sums, outer_cos, precision=precise)
        - jnp.einsum("mra,ma->mr", sin_sums, outer_sin, precision=precise)
    )
    imag_terms = -norm_scale * (
        jnp.einsum("mra,ma->mr", cos_sums, outer_sin, precision=precise)
        + jnp.einsum("mra,ma->mr", sin_sums, outer_cos, precision=precise)
    )
    cycle_terms = jnp.stack([real_terms, imag_terms], axis=1).astype(jnp.bfloat16)

    per_owner = cycle_terms.reshape(nblk, 1, chunk)
    returning = jnp.broadcast_to(per_owner, (nblk, nband, chunk)).reshape(nblk * nband, chunk)
    arrived = lax.all_to_all(returning, EVERY, split_axis=0, concat_axis=0, tiled=True)
    mode_terms = arrived.reshape(nblk, nband, orders_dev, parts, cycles_dev)
    mode_terms = mode_terms.transpose(2, 1, 3, 0, 4).reshape(orders_dev, nband * parts, cycles_all)
    harmonic = jnp.einsum(
        "sqr,srl->sql", mode_terms, legendre_here, preferred_element_type=jnp.float32
    ).reshape(orders_dev, nband, parts, width)
    summed = jnp.sum(beam_here[None, :, None, :] * harmonic, axis=1)

    image = prior_inverse[None, None, :] * direction + summed
    scaled_res = preconditioner[None, None, :] * residual
    scaled_image = preconditioner[None, None, :] * image
    products = jnp.stack(
        [residual * scaled_res, direction * image, scaled_res * image, scaled_image * image]
    )
    local_sums = jnp.sum(products.reshape(products.shape[0], -1), axis=1)
    shared = jnp.broadcast_to(local_sums[None], (nblk * nband, local_sums.shape[0]))
    arrived_sums = lax.all_to_all(shared, EVERY, split_axis=0, concat_axis=0, tiled=True)
    totals = lax.optimization_barrier(
        jnp.broadcast_to(
            jnp.sum(arrived_sums, axis=0)[:, None, None, None], (local_sums.shape[0], 1, 1, width)
        )
    )
    norm_now = totals[0]
    step_size = norm_now / totals[1]
    norm_next = norm_now - step_size * (2.0 * totals[2] - step_size * totals[3])
    residual_next = residual - step_size * image
    precond_next = preconditioner[None, None, :] * residual_next
    solution_next = solution + step_size * direction
    direction_next = precond_next + norm_next / norm_now * direction
    return (solution_next, residual_next, direction_next)


def solution(mesh):
    return jax.shard_map(
        per_device,
        mesh=mesh,
        in_specs=(
            P("blk", None, "band"),
            P("blk", None, "band"),
            P("blk", None, "band"),
            P("band"),
            P("band"),
            P("band", None),
            P("blk", None, None),
            P(),
            P("band", "blk", None),
            P(),
            P("blk"),
            P("blk"),
        ),
        out_specs=(P("blk", None, "band"), P("blk", None, "band"), P("blk", None, "band")),
        check_vma=False,
    )
```

```python
import math

import jax
import jax.numpy as jnp
from jax import lax
from jax.sharding import PartitionSpec as P

NPHI = 8192
TILE = 64


precise = lax.Precision.HIGHEST
EVERY = ("blk", "band")


def phases(mode_orders, column_count, stride):
    columns = jnp.arange(column_count, dtype=jnp.int32) * stride
    turn_counts = mode_orders[:, None] * columns[None, :] % NPHI
    angles = turn_counts.astype(jnp.float32) * (2.0 * math.pi / NPHI)
    return (jnp.cos(angles), jnp.sin(angles))


def pick_kind(per_kind, tile_kinds):
    kinds = jnp.arange(per_kind.shape[1], dtype=jnp.int32)
    chosen = tile_kinds[:, None, None] == kinds[None, :, None]
    return jnp.sum(jnp.where(chosen, per_kind, 0.0), axis=1)


def smooth(pixels, smoother_blocks, tile_slots, tile_kinds):
    tile_rows = pixels.reshape(-1, TILE)
    picked = tile_rows[tile_slots]
    inner_all = jnp.einsum("kij,tj->tki", smoother_blocks, picked, precision=precise)
    inner_part = pick_kind(inner_all, tile_kinds)
    outer_all = jnp.einsum("kji,tj->tki", smoother_blocks, inner_part, precision=precise)
    outer_part = pick_kind(outer_all, tile_kinds)
    return jnp.zeros_like(tile_rows).at[tile_slots].add(outer_part).reshape(pixels.shape)


def per_device(
    solution,
    residual,
    direction,
    prior_inverse,
    preconditioner,
    beam_window,
    legendre,
    mode_orders,
    noise_weight,
    smoother_blocks,
    tile_slots,
    tile_kinds,
):
    nblk = lax.axis_size("blk")
    nband = lax.axis_size("band")
    band = lax.axis_index("band")
    orders_dev, parts, width = direction.shape
    cycles_all = legendre.shape[1]
    cycles_dev = cycles_all // nblk
    order_count = mode_orders.shape[0]
    norm_scale = 1.0 / math.sqrt(order_count)

    beam_here = lax.all_to_all(
        beam_window.reshape(nband, width), "band", split_axis=0, concat_axis=0, tiled=True
    )
    legendre_here = lax.dynamic_slice_in_dim(legendre, band * width, width, 2)

    weighted = (beam_here[None, :, None, :] * direction[:, None, :, :]).astype(jnp.bfloat16)
    weighted = weighted.reshape(orders_dev, nband * parts, width)
    partial = jnp.einsum(
        "sql,srl->sqr", weighted, legendre_here, preferred_element_type=jnp.float32
    )
    partial = partial.reshape(orders_dev, nband, parts, nblk, cycles_dev)
    chunk = orders_dev * parts * cycles_dev
    outgoing = partial.transpose(3, 1, 0, 2, 4).reshape(nblk * nband, chunk)
    incoming = lax.all_to_all(outgoing, EVERY, split_axis=0, concat_axis=0, tiled=True)
    cycle_coefficients = jnp.sum(
        incoming.reshape(nblk, nband, orders_dev, parts, cycles_dev), axis=1
    ).reshape(order_count, parts, cycles_dev)

    cycle_count = cycles_dev
    outer_cos, outer_sin = phases(mode_orders, NPHI // 128, 128)
    inner_cos, inner_sin = phases(mode_orders, 128, 1)
    real_part = cycle_coefficients[:, 0, :, None]
    imag_part = cycle_coefficients[:, 1, :, None]
    upper_part = real_part * outer_cos[:, None, :] - imag_part * outer_sin[:, None, :]
    lower_part = real_part * outer_sin[:, None, :] + imag_part * outer_cos[:, None, :]
    inner_both = jnp.concatenate([inner_cos, inner_sin], axis=0)
    pixel_grid = jnp.einsum(
        "mra,mb->rab",
        jnp.concatenate([upper_part, -lower_part], axis=0),
        inner_both,
        precision=precise,
    )
    pixels = norm_scale * pixel_grid.reshape(cycle_count, NPHI)
    noisy = noise_weight[0] * pixels + smooth(pixels, smoother_blocks, tile_slots, tile_kinds)
    noisy_grid = noisy.reshape(cycle_count, NPHI // 128, 128)
    both_sums = jnp.einsum("rab,mb->mra", noisy_grid, inner_both, precision=precise)
    cos_sums, sin_sums = both_sums[:order_count], both_sums[order_count:]
    real_terms = norm_scale * (
        jnp.einsum("mra,ma->mr", cos_sums, outer_cos, precision=precise)
        - jnp.einsum("mra,ma->mr", sin_sums, outer_sin, precision=precise)
    )
    imag_terms = -norm_scale * (
        jnp.einsum("mra,ma->mr", cos_sums, outer_sin, precision=precise)
        + jnp.einsum("mra,ma->mr", sin_sums, outer_cos, precision=precise)
    )
    cycle_terms = jnp.stack([real_terms, imag_terms], axis=1).astype(jnp.bfloat16)

    per_owner = cycle_terms.reshape(nblk, 1, chunk)
    returning = jnp.broadcast_to(per_owner, (nblk, nband, chunk)).reshape(nblk * nband, chunk)
    arrived = lax.all_to_all(returning, EVERY, split_axis=0, concat_axis=0, tiled=True)
    mode_terms = arrived.reshape(nblk, nband, orders_dev, parts, cycles_dev)
    mode_terms = mode_terms.transpose(2, 1, 3, 0, 4).reshape(orders_dev, nband * parts, cycles_all)
    harmonic = jnp.einsum(
        "sqr,srl->sql", mode_terms, legendre_here, preferred_element_type=jnp.float32
    ).reshape(orders_dev, nband, parts, width)
    summed = jnp.sum(beam_here[None, :, None, :] * harmonic, axis=1)

    image = prior_inverse[None, None, :] * direction + summed
    scaled_res = preconditioner[None, None, :] * residual
    scaled_image = preconditioner[None, None, :] * image
    products = jnp.stack(
        [residual * scaled_res, direction * image, scaled_res * image, scaled_image * image]
    )
    local_sums = jnp.sum(products.reshape(products.shape[0], -1), axis=1)
    shared = jnp.broadcast_to(local_sums[None], (nblk * nband, local_sums.shape[0]))
    arrived_sums = lax.all_to_all(shared, EVERY, split_axis=0, concat_axis=0, tiled=True)
    totals = lax.optimization_barrier(
        jnp.broadcast_to(
            jnp.sum(arrived_sums, axis=0)[:, None, None, None], (local_sums.shape[0], 1, 1, width)
        )
    )
    norm_now = totals[0]
    step_size = norm_now / totals[1]
    norm_next = norm_now - step_size * (2.0 * totals[2] - step_size * totals[3])
    residual_next = residual - step_size * image
    precond_next = preconditioner[None, None, :] * residual_next
    solution_next = solution + step_size * direction
    direction_next = precond_next + norm_next / norm_now * direction
    return (solution_next, residual_next, direction_next)


def solution(mesh):
    return jax.shard_map(
        per_device,
        mesh=mesh,
        in_specs=(
            P("blk", None, "band"),
            P("blk", None, "band"),
            P("blk", None, "band"),
            P("band"),
            P("band"),
            P("band", None),
            P("blk", None, None),
            P(),
            P("band", "blk", None),
            P(),
            P("blk"),
            P("blk"),
        ),
        out_specs=(P("blk", None, "band"), P("blk", None, "band"), P("blk", None, "band")),
        check_vma=False,
    )
```

```python
import math

import jax
import jax.numpy as jnp
from jax import lax
from jax.sharding import PartitionSpec as P

NPHI = 8192
TILE = 64


precise = lax.Precision.HIGHEST
EVERY = ("blk", "band")


def phases(mode_orders, column_count, stride):
    columns = jnp.arange(column_count, dtype=jnp.int32) * stride
    turn_counts = mode_orders[:, None] * columns[None, :] % NPHI
    angles = turn_counts.astype(jnp.float32) * (2.0 * math.pi / NPHI)
    return (jnp.cos(angles), jnp.sin(angles))


def pick_kind(per_kind, tile_kinds):
    kinds = jnp.arange(per_kind.shape[1], dtype=jnp.int32)
    chosen = tile_kinds[:, None, None] == kinds[None, :, None]
    return jnp.sum(jnp.where(chosen, per_kind, 0.0), axis=1)


def smooth(pixels, smoother_blocks, tile_slots, tile_kinds):
    tile_rows = pixels.reshape(-1, TILE)
    picked = tile_rows[tile_slots]
    inner_all = jnp.einsum("kij,tj->tki", smoother_blocks, picked, precision=precise)
    inner_part = pick_kind(inner_all, tile_kinds)
    outer_all = jnp.einsum("kji,tj->tki", smoother_blocks, inner_part, precision=precise)
    outer_part = pick_kind(outer_all, tile_kinds)
    return jnp.zeros_like(tile_rows).at[tile_slots].add(outer_part).reshape(pixels.shape)


def per_device(
    solution,
    residual,
    direction,
    prior_inverse,
    preconditioner,
    beam_window,
    legendre,
    mode_orders,
    noise_weight,
    smoother_blocks,
    tile_slots,
    tile_kinds,
):
    nblk = lax.axis_size("blk")
    nband = lax.axis_size("band")
    band = lax.axis_index("band")
    orders_dev, parts, width = direction.shape
    cycles_all = legendre.shape[1]
    cycles_dev = cycles_all // nblk
    order_count = mode_orders.shape[0]
    norm_scale = 1.0 / math.sqrt(order_count)

    beam_here = lax.all_to_all(
        beam_window.reshape(nband, width), "band", split_axis=0, concat_axis=0, tiled=True
    )
    legendre_here = lax.dynamic_slice_in_dim(legendre, band * width, width, 2)

    weighted = (beam_here[None, :, None, :] * direction[:, None, :, :]).astype(jnp.bfloat16)
    weighted = weighted.reshape(orders_dev, nband * parts, width)
    partial = jnp.einsum(
        "sql,srl->sqr", weighted, legendre_here, preferred_element_type=jnp.float32
    )
    partial = partial.reshape(orders_dev, nband, parts, nblk, cycles_dev)
    chunk = orders_dev * parts * cycles_dev
    outgoing = partial.transpose(3, 1, 0, 2, 4).reshape(nblk * nband, chunk)
    outer_cos, outer_sin = phases(mode_orders, NPHI // 128, 128)
    inner_cos, inner_sin = phases(mode_orders, 128, 1)
    outgoing, outer_cos, outer_sin, inner_cos, inner_sin = lax.optimization_barrier(
        (outgoing, outer_cos, outer_sin, inner_cos, inner_sin)
    )
    incoming = lax.all_to_all(outgoing, EVERY, split_axis=0, concat_axis=0, tiled=True)
    (
        incoming, outer_cos, outer_sin, inner_cos, inner_sin, tile_slots, tile_kinds,
        smoother_blocks, noise_weight, solution, residual, direction, prior_inverse,
        preconditioner, legendre_here, beam_here,
    ) = lax.optimization_barrier(
        (
            incoming, outer_cos, outer_sin, inner_cos, inner_sin, tile_slots, tile_kinds,
            smoother_blocks, noise_weight, solution, residual, direction, prior_inverse,
            preconditioner, legendre_here, beam_here,
        )
    )
    cycle_coefficients = jnp.sum(
        incoming.reshape(nblk, nband, orders_dev, parts, cycles_dev), axis=1
    ).reshape(order_count, parts, cycles_dev)

    cycle_count = cycles_dev
    real_part = cycle_coefficients[:, 0, :, None]
    imag_part = cycle_coefficients[:, 1, :, None]
    upper_part = real_part * outer_cos[:, None, :] - imag_part * outer_sin[:, None, :]
    lower_part = real_part * outer_sin[:, None, :] + imag_part * outer_cos[:, None, :]
    pixel_grid = jnp.einsum("mra,mb->rab", upper_part, inner_cos, precision=precise) - jnp.einsum(
        "mra,mb->rab", lower_part, inner_sin, precision=precise
    )
    pixels = norm_scale * pixel_grid.reshape(cycle_count, NPHI)
    noisy = noise_weight[0] * pixels + smooth(pixels, smoother_blocks, tile_slots, tile_kinds)
    noisy_grid = noisy.reshape(cycle_count, NPHI // 128, 128)
    cos_sums = jnp.einsum("rab,mb->mra", noisy_grid, inner_cos, precision=precise)
    sin_sums = jnp.einsum("rab,mb->mra", noisy_grid, inner_sin, precision=precise)
    real_terms = norm_scale * (
        jnp.einsum("mra,ma->mr", cos_sums, outer_cos, precision=precise)
        - jnp.einsum("mra,ma->mr", sin_sums, outer_sin, precision=precise)
    )
    imag_terms = -norm_scale * (
        jnp.einsum("mra,ma->mr", cos_sums, outer_sin, precision=precise)
        + jnp.einsum("mra,ma->mr", sin_sums, outer_cos, precision=precise)
    )
    cycle_terms = jnp.stack([real_terms, imag_terms], axis=1).astype(jnp.bfloat16)

    per_owner = cycle_terms.reshape(nblk, 1, chunk)
    returning = jnp.broadcast_to(per_owner, (nblk, nband, chunk)).reshape(nblk * nband, chunk)
    arrived = lax.all_to_all(returning, EVERY, split_axis=0, concat_axis=0, tiled=True)
    mode_terms = arrived.reshape(nblk, nband, orders_dev, parts, cycles_dev)
    mode_terms = mode_terms.transpose(2, 1, 3, 0, 4).reshape(orders_dev, nband * parts, cycles_all)
    harmonic = jnp.einsum(
        "sqr,srl->sql", mode_terms, legendre_here, preferred_element_type=jnp.float32
    ).reshape(orders_dev, nband, parts, width)
    summed = jnp.sum(beam_here[None, :, None, :] * harmonic, axis=1)

    image = prior_inverse[None, None, :] * direction + summed
    scaled_res = preconditioner[None, None, :] * residual
    scaled_image = preconditioner[None, None, :] * image
    products = jnp.stack(
        [residual * scaled_res, direction * image, scaled_res * image, scaled_image * image]
    )
    local_sums = jnp.sum(products.reshape(products.shape[0], -1), axis=1)
    shared = jnp.broadcast_to(local_sums[None], (nblk * nband, local_sums.shape[0]))
    arrived_sums = lax.all_to_all(shared, EVERY, split_axis=0, concat_axis=0, tiled=True)
    totals = lax.optimization_barrier(
        jnp.broadcast_to(
            jnp.sum(arrived_sums, axis=0)[:, None, None, None], (local_sums.shape[0], 1, 1, width)
        )
    )
    norm_now = totals[0]
    step_size = norm_now / totals[1]
    norm_next = norm_now - step_size * (2.0 * totals[2] - step_size * totals[3])
    residual_next = residual - step_size * image
    precond_next = preconditioner[None, None, :] * residual_next
    solution_next = solution + step_size * direction
    direction_next = precond_next + norm_next / norm_now * direction
    return (solution_next, residual_next, direction_next)


def solution(mesh):
    return jax.shard_map(
        per_device,
        mesh=mesh,
        in_specs=(
            P("blk", None, "band"),
            P("blk", None, "band"),
            P("blk", None, "band"),
            P("band"),
            P("band"),
            P("band", None),
            P("blk", None, None),
            P(),
            P("band", "blk", None),
            P(),
            P("blk"),
            P("blk"),
        ),
        out_specs=(P("blk", None, "band"), P("blk", None, "band"), P("blk", None, "band")),
        check_vma=False,
    )
```

```python
import math

import jax
import jax.numpy as jnp
from jax import lax
from jax.sharding import PartitionSpec as P

NPHI = 8192
TILE = 64


precise = lax.Precision.HIGHEST
EVERY = ("blk", "band")


def phases(mode_orders, column_count, stride):
    columns = jnp.arange(column_count, dtype=jnp.int32) * stride
    turn_counts = mode_orders[:, None] * columns[None, :] % NPHI
    angles = turn_counts.astype(jnp.float32) * (2.0 * math.pi / NPHI)
    return (jnp.cos(angles), jnp.sin(angles))


def pick_kind(per_kind, tile_kinds):
    kinds = jnp.arange(per_kind.shape[1], dtype=jnp.int32)
    chosen = tile_kinds[:, None, None] == kinds[None, :, None]
    return jnp.sum(jnp.where(chosen, per_kind, 0.0), axis=1)


def smooth(pixels, smoother_blocks, tile_slots, tile_kinds):
    tile_rows = pixels.reshape(-1, TILE)
    picked = tile_rows[tile_slots]
    inner_all = jnp.einsum("kij,tj->tki", smoother_blocks, picked, precision=precise)
    inner_part = pick_kind(inner_all, tile_kinds)
    outer_all = jnp.einsum("kji,tj->tki", smoother_blocks, inner_part, precision=precise)
    outer_part = pick_kind(outer_all, tile_kinds)
    return jnp.zeros_like(tile_rows).at[tile_slots].add(outer_part).reshape(pixels.shape)


def per_device(
    solution,
    residual,
    direction,
    prior_inverse,
    preconditioner,
    beam_window,
    legendre,
    mode_orders,
    noise_weight,
    smoother_blocks,
    tile_slots,
    tile_kinds,
):
    nblk = lax.axis_size("blk")
    nband = lax.axis_size("band")
    band = lax.axis_index("band")
    orders_dev, parts, width = direction.shape
    cycles_all = legendre.shape[1]
    cycles_dev = cycles_all // nblk
    order_count = mode_orders.shape[0]
    norm_scale = 1.0 / math.sqrt(order_count)

    beam_here = lax.all_to_all(
        beam_window.reshape(nband, width), "band", split_axis=0, concat_axis=0, tiled=True
    )
    legendre_here = lax.dynamic_slice_in_dim(legendre, band * width, width, 2)

    weighted = (beam_here[None, :, None, :] * direction[:, None, :, :]).astype(jnp.bfloat16)
    weighted = weighted.reshape(orders_dev, nband * parts, width)
    partial = jnp.einsum(
        "sql,srl->sqr", weighted, legendre_here, preferred_element_type=jnp.float32
    )
    partial = partial.reshape(orders_dev, nband, parts, nblk, cycles_dev)
    chunk = orders_dev * parts * cycles_dev
    outgoing = partial.transpose(3, 1, 0, 2, 4).reshape(nblk * nband, chunk)
    high = outgoing.astype(jnp.bfloat16)
    low = (outgoing - high.astype(jnp.float32)).astype(jnp.bfloat16)
    pair = lax.all_to_all(
        jnp.concatenate([high, low], axis=1), EVERY, split_axis=0, concat_axis=0, tiled=True
    )
    incoming = pair[:, :chunk].astype(jnp.float32) + pair[:, chunk:].astype(jnp.float32)
    cycle_coefficients = jnp.sum(
        incoming.reshape(nblk, nband, orders_dev, parts, cycles_dev), axis=1
    ).reshape(order_count, parts, cycles_dev)

    cycle_count = cycles_dev
    outer_cos, outer_sin = phases(mode_orders, NPHI // 128, 128)
    inner_cos, inner_sin = phases(mode_orders, 128, 1)
    real_part = cycle_coefficients[:, 0, :, None]
    imag_part = cycle_coefficients[:, 1, :, None]
    upper_part = real_part * outer_cos[:, None, :] - imag_part * outer_sin[:, None, :]
    lower_part = real_part * outer_sin[:, None, :] + imag_part * outer_cos[:, None, :]
    pixel_grid = jnp.einsum("mra,mb->rab", upper_part, inner_cos, precision=precise) - jnp.einsum(
        "mra,mb->rab", lower_part, inner_sin, precision=precise
    )
    pixels = norm_scale * pixel_grid.reshape(cycle_count, NPHI)
    noisy = noise_weight[0] * pixels + smooth(pixels, smoother_blocks, tile_slots, tile_kinds)
    noisy_grid = noisy.reshape(cycle_count, NPHI // 128, 128)
    cos_sums = jnp.einsum("rab,mb->mra", noisy_grid, inner_cos, precision=precise)
    sin_sums = jnp.einsum("rab,mb->mra", noisy_grid, inner_sin, precision=precise)
    real_terms = norm_scale * (
        jnp.einsum("mra,ma->mr", cos_sums, outer_cos, precision=precise)
        - jnp.einsum("mra,ma->mr", sin_sums, outer_sin, precision=precise)
    )
    imag_terms = -norm_scale * (
        jnp.einsum("mra,ma->mr", cos_sums, outer_sin, precision=precise)
        + jnp.einsum("mra,ma->mr", sin_sums, outer_cos, precision=precise)
    )
    cycle_terms = jnp.stack([real_terms, imag_terms], axis=1).astype(jnp.bfloat16)

    per_owner = cycle_terms.reshape(nblk, 1, chunk)
    returning = jnp.broadcast_to(per_owner, (nblk, nband, chunk)).reshape(nblk * nband, chunk)
    arrived = lax.all_to_all(returning, EVERY, split_axis=0, concat_axis=0, tiled=True)
    mode_terms = arrived.reshape(nblk, nband, orders_dev, parts, cycles_dev)
    mode_terms = mode_terms.transpose(2, 1, 3, 0, 4).reshape(orders_dev, nband * parts, cycles_all)
    harmonic = jnp.einsum(
        "sqr,srl->sql", mode_terms, legendre_here, preferred_element_type=jnp.float32
    ).reshape(orders_dev, nband, parts, width)
    summed = jnp.sum(beam_here[None, :, None, :] * harmonic, axis=1)

    image = prior_inverse[None, None, :] * direction + summed
    scaled_res = preconditioner[None, None, :] * residual
    scaled_image = preconditioner[None, None, :] * image
    products = jnp.stack(
        [residual * scaled_res, direction * image, scaled_res * image, scaled_image * image]
    )
    local_sums = jnp.sum(products.reshape(products.shape[0], -1), axis=1)
    shared = jnp.broadcast_to(local_sums[None], (nblk * nband, local_sums.shape[0]))
    arrived_sums = lax.all_to_all(shared, EVERY, split_axis=0, concat_axis=0, tiled=True)
    totals = lax.optimization_barrier(
        jnp.broadcast_to(
            jnp.sum(arrived_sums, axis=0)[:, None, None, None], (local_sums.shape[0], 1, 1, width)
        )
    )
    norm_now = totals[0]
    step_size = norm_now / totals[1]
    norm_next = norm_now - step_size * (2.0 * totals[2] - step_size * totals[3])
    residual_next = residual - step_size * image
    precond_next = preconditioner[None, None, :] * residual_next
    solution_next = solution + step_size * direction
    direction_next = precond_next + norm_next / norm_now * direction
    return (solution_next, residual_next, direction_next)


def solution(mesh):
    return jax.shard_map(
        per_device,
        mesh=mesh,
        in_specs=(
            P("blk", None, "band"),
            P("blk", None, "band"),
            P("blk", None, "band"),
            P("band"),
            P("band"),
            P("band", None),
            P("blk", None, None),
            P(),
            P("band", "blk", None),
            P(),
            P("blk"),
            P("blk"),
        ),
        out_specs=(P("blk", None, "band"), P("blk", None, "band"), P("blk", None, "band")),
        check_vma=False,
    )
```

```python
import math

import jax
import jax.numpy as jnp
from jax import lax
from jax.sharding import PartitionSpec as P

NPHI = 8192
TILE = 64


precise = lax.Precision.HIGHEST
EVERY = ("blk", "band")


def phases(mode_orders, column_count, stride):
    columns = jnp.arange(column_count, dtype=jnp.int32) * stride
    turn_counts = mode_orders[:, None] * columns[None, :] % NPHI
    angles = turn_counts.astype(jnp.float32) * (2.0 * math.pi / NPHI)
    return (jnp.cos(angles), jnp.sin(angles))


def pick_kind(per_kind, tile_kinds):
    kinds = jnp.arange(per_kind.shape[1], dtype=jnp.int32)
    chosen = tile_kinds[:, None, None] == kinds[None, :, None]
    return jnp.sum(jnp.where(chosen, per_kind, 0.0), axis=1)


def smooth(pixels, smoother_blocks, tile_slots, tile_kinds):
    tile_rows = pixels.reshape(-1, TILE)
    picked = tile_rows[tile_slots]
    inner_all = jnp.einsum("kij,tj->tki", smoother_blocks, picked, precision=precise)
    inner_part = pick_kind(inner_all, tile_kinds)
    outer_all = jnp.einsum("kji,tj->tki", smoother_blocks, inner_part, precision=precise)
    outer_part = pick_kind(outer_all, tile_kinds)
    return jnp.zeros_like(tile_rows).at[tile_slots].add(outer_part).reshape(pixels.shape)


def per_device(
    solution,
    residual,
    direction,
    prior_inverse,
    preconditioner,
    beam_window,
    legendre,
    mode_orders,
    noise_weight,
    smoother_blocks,
    tile_slots,
    tile_kinds,
):
    nblk = lax.axis_size("blk")
    nband = lax.axis_size("band")
    band = lax.axis_index("band")
    orders_dev, parts, width = direction.shape
    cycles_all = legendre.shape[1]
    cycles_dev = cycles_all // nblk
    order_count = mode_orders.shape[0]
    norm_scale = 1.0 / math.sqrt(order_count)

    sub = orders_dev // nband
    multipoles = width * nband
    direction_rows = direction.reshape(nband, sub * parts * width)
    beam_rows = jnp.broadcast_to(beam_window.reshape(1, multipoles), (nband, multipoles))
    arrived_rows = lax.all_to_all(
        jnp.concatenate([direction_rows, beam_rows], axis=1), "band", 0, 0, tiled=True
    )
    direction_share = (
        arrived_rows[:, : sub * parts * width]
        .reshape(nband, sub, parts, width)
        .transpose(1, 2, 0, 3)
        .reshape(sub, parts, multipoles)
    )
    beam_all = arrived_rows[:, sub * parts * width :]
    beam_here = lax.dynamic_slice_in_dim(beam_all, band * width, width, 1)
    legendre_here = lax.dynamic_slice_in_dim(legendre, band * width, width, 2)
    legendre_share = lax.dynamic_slice_in_dim(legendre, band * sub, sub, 0)

    weighted = (beam_all[None, :, None, :] * direction_share[:, None, :, :]).astype(jnp.bfloat16)
    weighted = weighted.reshape(sub, nband * parts, multipoles)
    coefficients = jnp.einsum(
        "sql,srl->sqr", weighted, legendre_share, preferred_element_type=jnp.float32
    )
    coefficients = coefficients.reshape(sub, nband, parts, nblk, cycles_dev)
    chunk = sub * parts * cycles_dev
    outgoing = coefficients.transpose(3, 1, 0, 2, 4).reshape(nblk * nband, chunk)
    incoming = lax.all_to_all(outgoing, EVERY, split_axis=0, concat_axis=0, tiled=True)
    cycle_coefficients = incoming.reshape(order_count, parts, cycles_dev)

    cycle_count = cycles_dev
    outer_cos, outer_sin = phases(mode_orders, NPHI // 128, 128)
    inner_cos, inner_sin = phases(mode_orders, 128, 1)
    real_part = cycle_coefficients[:, 0, :, None]
    imag_part = cycle_coefficients[:, 1, :, None]
    upper_part = real_part * outer_cos[:, None, :] - imag_part * outer_sin[:, None, :]
    lower_part = real_part * outer_sin[:, None, :] + imag_part * outer_cos[:, None, :]
    pixel_grid = jnp.einsum("mra,mb->rab", upper_part, inner_cos, precision=precise) - jnp.einsum(
        "mra,mb->rab", lower_part, inner_sin, precision=precise
    )
    pixels = norm_scale * pixel_grid.reshape(cycle_count, NPHI)
    noisy = noise_weight[0] * pixels + smooth(pixels, smoother_blocks, tile_slots, tile_kinds)
    noisy_grid = noisy.reshape(cycle_count, NPHI // 128, 128)
    cos_sums = jnp.einsum("rab,mb->mra", noisy_grid, inner_cos, precision=precise)
    sin_sums = jnp.einsum("rab,mb->mra", noisy_grid, inner_sin, precision=precise)
    real_terms = norm_scale * (
        jnp.einsum("mra,ma->mr", cos_sums, outer_cos, precision=precise)
        - jnp.einsum("mra,ma->mr", sin_sums, outer_sin, precision=precise)
    )
    imag_terms = -norm_scale * (
        jnp.einsum("mra,ma->mr", cos_sums, outer_sin, precision=precise)
        + jnp.einsum("mra,ma->mr", sin_sums, outer_cos, precision=precise)
    )
    cycle_terms = jnp.stack([real_terms, imag_terms], axis=1).astype(jnp.bfloat16)

    back_chunk = orders_dev * parts * cycles_dev
    per_owner = cycle_terms.reshape(nblk, 1, back_chunk)
    returning = jnp.broadcast_to(per_owner, (nblk, nband, back_chunk)).reshape(
        nblk * nband, back_chunk
    )
    arrived = lax.all_to_all(returning, EVERY, split_axis=0, concat_axis=0, tiled=True)
    mode_terms = arrived.reshape(nblk, nband, orders_dev, parts, cycles_dev)
    mode_terms = mode_terms.transpose(2, 1, 3, 0, 4).reshape(orders_dev, nband * parts, cycles_all)
    harmonic = jnp.einsum(
        "sqr,srl->sql", mode_terms, legendre_here, preferred_element_type=jnp.float32
    ).reshape(orders_dev, nband, parts, width)
    summed = jnp.sum(beam_here[None, :, None, :] * harmonic, axis=1)

    image = prior_inverse[None, None, :] * direction + summed
    scaled_res = preconditioner[None, None, :] * residual
    scaled_image = preconditioner[None, None, :] * image
    products = jnp.stack(
        [residual * scaled_res, direction * image, scaled_res * image, scaled_image * image]
    )
    local_sums = jnp.sum(products.reshape(products.shape[0], -1), axis=1)
    shared = jnp.broadcast_to(local_sums[None], (nblk * nband, local_sums.shape[0]))
    arrived_sums = lax.all_to_all(shared, EVERY, split_axis=0, concat_axis=0, tiled=True)
    totals = lax.optimization_barrier(
        jnp.broadcast_to(
            jnp.sum(arrived_sums, axis=0)[:, None, None, None], (local_sums.shape[0], 1, 1, width)
        )
    )
    norm_now = totals[0]
    step_size = norm_now / totals[1]
    norm_next = norm_now - step_size * (2.0 * totals[2] - step_size * totals[3])
    residual_next = residual - step_size * image
    precond_next = preconditioner[None, None, :] * residual_next
    solution_next = solution + step_size * direction
    direction_next = precond_next + norm_next / norm_now * direction
    return (solution_next, residual_next, direction_next)


def solution(mesh):
    return jax.shard_map(
        per_device,
        mesh=mesh,
        in_specs=(
            P("blk", None, "band"),
            P("blk", None, "band"),
            P("blk", None, "band"),
            P("band"),
            P("band"),
            P("band", None),
            P("blk", None, None),
            P(),
            P("band", "blk", None),
            P(),
            P("blk"),
            P("blk"),
        ),
        out_specs=(P("blk", None, "band"), P("blk", None, "band"), P("blk", None, "band")),
        check_vma=False,
    )
```

```python
import math

import jax
import jax.numpy as jnp
from jax import lax
from jax.sharding import PartitionSpec as P

NPHI = 8192
TILE = 64


precise = lax.Precision.HIGH
EVERY = ("blk", "band")


def phases(mode_orders, column_count, stride):
    columns = jnp.arange(column_count, dtype=jnp.int32) * stride
    turn_counts = mode_orders[:, None] * columns[None, :] % NPHI
    angles = turn_counts.astype(jnp.float32) * (2.0 * math.pi / NPHI)
    return (jnp.cos(angles), jnp.sin(angles))


def pick_kind(per_kind, tile_kinds):
    kinds = jnp.arange(per_kind.shape[1], dtype=jnp.int32)
    chosen = tile_kinds[:, None, None] == kinds[None, :, None]
    return jnp.sum(jnp.where(chosen, per_kind, 0.0), axis=1)


def smooth(pixels, smoother_blocks, tile_slots, tile_kinds):
    tile_rows = pixels.reshape(-1, TILE)
    picked = tile_rows[tile_slots]
    inner_all = jnp.einsum("kij,tj->tki", smoother_blocks, picked, precision=precise)
    inner_part = pick_kind(inner_all, tile_kinds)
    outer_all = jnp.einsum("kji,tj->tki", smoother_blocks, inner_part, precision=precise)
    outer_part = pick_kind(outer_all, tile_kinds)
    return jnp.zeros_like(tile_rows).at[tile_slots].add(outer_part).reshape(pixels.shape)


def per_device(
    solution,
    residual,
    direction,
    prior_inverse,
    preconditioner,
    beam_window,
    legendre,
    mode_orders,
    noise_weight,
    smoother_blocks,
    tile_slots,
    tile_kinds,
):
    nblk = lax.axis_size("blk")
    nband = lax.axis_size("band")
    band = lax.axis_index("band")
    orders_dev, parts, width = direction.shape
    cycles_all = legendre.shape[1]
    cycles_dev = cycles_all // nblk
    order_count = mode_orders.shape[0]
    norm_scale = 1.0 / math.sqrt(order_count)

    beam_here = lax.all_to_all(
        beam_window.reshape(nband, width), "band", split_axis=0, concat_axis=0, tiled=True
    )
    legendre_here = lax.dynamic_slice_in_dim(legendre, band * width, width, 2)

    weighted = (beam_here[None, :, None, :] * direction[:, None, :, :]).astype(jnp.bfloat16)
    weighted = weighted.reshape(orders_dev, nband * parts, width)
    partial = jnp.einsum(
        "sql,srl->sqr", weighted, legendre_here, preferred_element_type=jnp.float32
    )
    partial = partial.reshape(orders_dev, nband, parts, nblk, cycles_dev)
    chunk = orders_dev * parts * cycles_dev
    outgoing = partial.transpose(3, 1, 0, 2, 4).reshape(nblk * nband, chunk)
    incoming = lax.all_to_all(outgoing, EVERY, split_axis=0, concat_axis=0, tiled=True)
    cycle_coefficients = jnp.sum(
        incoming.reshape(nblk, nband, orders_dev, parts, cycles_dev), axis=1
    ).reshape(order_count, parts, cycles_dev)

    cycle_count = cycles_dev
    outer_cos, outer_sin = phases(mode_orders, NPHI // 128, 128)
    inner_cos, inner_sin = phases(mode_orders, 128, 1)
    real_part = cycle_coefficients[:, 0, :, None]
    imag_part = cycle_coefficients[:, 1, :, None]
    upper_part = real_part * outer_cos[:, None, :] - imag_part * outer_sin[:, None, :]
    lower_part = real_part * outer_sin[:, None, :] + imag_part * outer_cos[:, None, :]
    pixel_grid = jnp.einsum("mra,mb->rab", upper_part, inner_cos, precision=precise) - jnp.einsum(
        "mra,mb->rab", lower_part, inner_sin, precision=precise
    )
    pixels = norm_scale * pixel_grid.reshape(cycle_count, NPHI)
    noisy = noise_weight[0] * pixels + smooth(pixels, smoother_blocks, tile_slots, tile_kinds)
    noisy_grid = noisy.reshape(cycle_count, NPHI // 128, 128)
    cos_sums = jnp.einsum("rab,mb->mra", noisy_grid, inner_cos, precision=precise)
    sin_sums = jnp.einsum("rab,mb->mra", noisy_grid, inner_sin, precision=precise)
    real_terms = norm_scale * (
        jnp.einsum("mra,ma->mr", cos_sums, outer_cos, precision=precise)
        - jnp.einsum("mra,ma->mr", sin_sums, outer_sin, precision=precise)
    )
    imag_terms = -norm_scale * (
        jnp.einsum("mra,ma->mr", cos_sums, outer_sin, precision=precise)
        + jnp.einsum("mra,ma->mr", sin_sums, outer_cos, precision=precise)
    )
    cycle_terms = jnp.stack([real_terms, imag_terms], axis=1).astype(jnp.bfloat16)

    per_owner = cycle_terms.reshape(nblk, 1, chunk)
    returning = jnp.broadcast_to(per_owner, (nblk, nband, chunk)).reshape(nblk * nband, chunk)
    arrived = lax.all_to_all(returning, EVERY, split_axis=0, concat_axis=0, tiled=True)
    mode_terms = arrived.reshape(nblk, nband, orders_dev, parts, cycles_dev)
    mode_terms = mode_terms.transpose(2, 1, 3, 0, 4).reshape(orders_dev, nband * parts, cycles_all)
    harmonic = jnp.einsum(
        "sqr,srl->sql", mode_terms, legendre_here, preferred_element_type=jnp.float32
    ).reshape(orders_dev, nband, parts, width)
    summed = jnp.sum(beam_here[None, :, None, :] * harmonic, axis=1)

    image = prior_inverse[None, None, :] * direction + summed
    scaled_res = preconditioner[None, None, :] * residual
    scaled_image = preconditioner[None, None, :] * image
    products = jnp.stack(
        [residual * scaled_res, direction * image, scaled_res * image, scaled_image * image]
    )
    local_sums = jnp.sum(products.reshape(products.shape[0], -1), axis=1)
    shared = jnp.broadcast_to(local_sums[None], (nblk * nband, local_sums.shape[0]))
    arrived_sums = lax.all_to_all(shared, EVERY, split_axis=0, concat_axis=0, tiled=True)
    totals = lax.optimization_barrier(
        jnp.broadcast_to(
            jnp.sum(arrived_sums, axis=0)[:, None, None, None], (local_sums.shape[0], 1, 1, width)
        )
    )
    norm_now = totals[0]
    step_size = norm_now / totals[1]
    norm_next = norm_now - step_size * (2.0 * totals[2] - step_size * totals[3])
    residual_next = residual - step_size * image
    precond_next = preconditioner[None, None, :] * residual_next
    solution_next = solution + step_size * direction
    direction_next = precond_next + norm_next / norm_now * direction
    return (solution_next, residual_next, direction_next)


def solution(mesh):
    return jax.shard_map(
        per_device,
        mesh=mesh,
        in_specs=(
            P("blk", None, "band"),
            P("blk", None, "band"),
            P("blk", None, "band"),
            P("band"),
            P("band"),
            P("band", None),
            P("blk", None, None),
            P(),
            P("band", "blk", None),
            P(),
            P("blk"),
            P("blk"),
        ),
        out_specs=(P("blk", None, "band"), P("blk", None, "band"), P("blk", None, "band")),
        check_vma=False,
    )
```

```python
import math

import jax
import jax.numpy as jnp
from jax import lax
from jax.sharding import PartitionSpec as P

NPHI = 8192
TILE = 64


precise = lax.Precision.HIGH
EVERY = ("blk", "band")


def phases(mode_orders, column_count, stride):
    columns = jnp.arange(column_count, dtype=jnp.int32) * stride
    turn_counts = mode_orders[:, None] * columns[None, :] % NPHI
    angles = turn_counts.astype(jnp.float32) * (2.0 * math.pi / NPHI)
    return (jnp.cos(angles), jnp.sin(angles))


def pick_kind(per_kind, tile_kinds):
    kinds = jnp.arange(per_kind.shape[1], dtype=jnp.int32)
    chosen = tile_kinds[:, None, None] == kinds[None, :, None]
    return jnp.sum(jnp.where(chosen, per_kind, 0.0), axis=1)


def smooth(pixels, smoother_blocks, tile_slots, tile_kinds):
    tile_rows = pixels.reshape(-1, TILE)
    picked = tile_rows[tile_slots]
    inner_all = jnp.einsum("kij,tj->tki", smoother_blocks, picked, precision=precise)
    inner_part = pick_kind(inner_all, tile_kinds)
    outer_all = jnp.einsum("kji,tj->tki", smoother_blocks, inner_part, precision=precise)
    outer_part = pick_kind(outer_all, tile_kinds)
    rows = jnp.arange(tile_rows.shape[0], dtype=jnp.int32)
    placed = (rows[:, None] == tile_slots[None, :]).astype(jnp.float32)
    spread = jnp.dot(placed, outer_part, precision=lax.Precision.HIGHEST)
    return spread.reshape(pixels.shape)


def per_device(
    solution,
    residual,
    direction,
    prior_inverse,
    preconditioner,
    beam_window,
    legendre,
    mode_orders,
    noise_weight,
    smoother_blocks,
    tile_slots,
    tile_kinds,
):
    nblk = lax.axis_size("blk")
    nband = lax.axis_size("band")
    band = lax.axis_index("band")
    orders_dev, parts, width = direction.shape
    cycles_all = legendre.shape[1]
    cycles_dev = cycles_all // nblk
    order_count = mode_orders.shape[0]
    norm_scale = 1.0 / math.sqrt(order_count)

    beam_here = lax.all_to_all(
        beam_window.reshape(nband, width), "band", split_axis=0, concat_axis=0, tiled=True
    )
    legendre_here = lax.dynamic_slice_in_dim(legendre, band * width, width, 2)

    weighted = (beam_here[None, :, None, :] * direction[:, None, :, :]).astype(jnp.bfloat16)
    weighted = weighted.reshape(orders_dev, nband * parts, width)
    partial = jnp.einsum(
        "sql,srl->sqr", weighted, legendre_here, preferred_element_type=jnp.float32
    )
    partial = partial.reshape(orders_dev, nband, parts, nblk, cycles_dev)
    chunk = orders_dev * parts * cycles_dev
    outgoing = partial.transpose(3, 1, 0, 2, 4).reshape(nblk * nband, chunk)
    incoming = lax.all_to_all(outgoing, EVERY, split_axis=0, concat_axis=0, tiled=True)
    cycle_coefficients = jnp.sum(
        incoming.reshape(nblk, nband, orders_dev, parts, cycles_dev), axis=1
    ).reshape(order_count, parts, cycles_dev)

    cycle_count = cycles_dev
    outer_cos, outer_sin = phases(mode_orders, NPHI // 128, 128)
    inner_cos, inner_sin = phases(mode_orders, 128, 1)
    real_part = cycle_coefficients[:, 0, :, None]
    imag_part = cycle_coefficients[:, 1, :, None]
    upper_part = real_part * outer_cos[:, None, :] - imag_part * outer_sin[:, None, :]
    lower_part = real_part * outer_sin[:, None, :] + imag_part * outer_cos[:, None, :]
    pixel_grid = jnp.einsum("mra,mb->rab", upper_part, inner_cos, precision=precise) - jnp.einsum(
        "mra,mb->rab", lower_part, inner_sin, precision=precise
    )
    pixels = norm_scale * pixel_grid.reshape(cycle_count, NPHI)
    noisy = noise_weight[0] * pixels + smooth(pixels, smoother_blocks, tile_slots, tile_kinds)
    noisy_grid = noisy.reshape(cycle_count, NPHI // 128, 128)
    cos_sums = jnp.einsum("rab,mb->mra", noisy_grid, inner_cos, precision=precise)
    sin_sums = jnp.einsum("rab,mb->mra", noisy_grid, inner_sin, precision=precise)
    real_terms = norm_scale * (
        jnp.einsum("mra,ma->mr", cos_sums, outer_cos, precision=precise)
        - jnp.einsum("mra,ma->mr", sin_sums, outer_sin, precision=precise)
    )
    imag_terms = -norm_scale * (
        jnp.einsum("mra,ma->mr", cos_sums, outer_sin, precision=precise)
        + jnp.einsum("mra,ma->mr", sin_sums, outer_cos, precision=precise)
    )
    cycle_terms = jnp.stack([real_terms, imag_terms], axis=1).astype(jnp.bfloat16)

    per_owner = cycle_terms.reshape(nblk, 1, chunk)
    returning = jnp.broadcast_to(per_owner, (nblk, nband, chunk)).reshape(nblk * nband, chunk)
    arrived = lax.all_to_all(returning, EVERY, split_axis=0, concat_axis=0, tiled=True)
    mode_terms = arrived.reshape(nblk, nband, orders_dev, parts, cycles_dev)
    mode_terms = mode_terms.transpose(2, 1, 3, 0, 4).reshape(orders_dev, nband * parts, cycles_all)
    harmonic = jnp.einsum(
        "sqr,srl->sql", mode_terms, legendre_here, preferred_element_type=jnp.float32
    ).reshape(orders_dev, nband, parts, width)
    summed = jnp.sum(beam_here[None, :, None, :] * harmonic, axis=1)

    image = prior_inverse[None, None, :] * direction + summed
    scaled_res = preconditioner[None, None, :] * residual
    scaled_image = preconditioner[None, None, :] * image
    products = jnp.stack(
        [residual * scaled_res, direction * image, scaled_res * image, scaled_image * image]
    )
    local_sums = jnp.sum(products.reshape(products.shape[0], -1), axis=1)
    shared = jnp.broadcast_to(local_sums[None], (nblk * nband, local_sums.shape[0]))
    arrived_sums = lax.all_to_all(shared, EVERY, split_axis=0, concat_axis=0, tiled=True)
    totals = lax.optimization_barrier(
        jnp.broadcast_to(
            jnp.sum(arrived_sums, axis=0)[:, None, None, None], (local_sums.shape[0], 1, 1, width)
        )
    )
    norm_now = totals[0]
    step_size = norm_now / totals[1]
    norm_next = norm_now - step_size * (2.0 * totals[2] - step_size * totals[3])
    residual_next = residual - step_size * image
    precond_next = preconditioner[None, None, :] * residual_next
    solution_next = solution + step_size * direction
    direction_next = precond_next + norm_next / norm_now * direction
    return (solution_next, residual_next, direction_next)


def solution(mesh):
    return jax.shard_map(
        per_device,
        mesh=mesh,
        in_specs=(
            P("blk", None, "band"),
            P("blk", None, "band"),
            P("blk", None, "band"),
            P("band"),
            P("band"),
            P("band", None),
            P("blk", None, None),
            P(),
            P("band", "blk", None),
            P(),
            P("blk"),
            P("blk"),
        ),
        out_specs=(P("blk", None, "band"), P("blk", None, "band"), P("blk", None, "band")),
        check_vma=False,
    )
```

```python
import math

import jax
import jax.numpy as jnp
from jax import lax
from jax.sharding import PartitionSpec as P

NPHI = 8192
TILE = 64


precise = lax.Precision.HIGH
EVERY = ("blk", "band")


def phases(mode_orders, column_count, stride):
    columns = jnp.arange(column_count, dtype=jnp.int32) * stride
    turn_counts = mode_orders[:, None] * columns[None, :] % NPHI
    angles = turn_counts.astype(jnp.float32) * (2.0 * math.pi / NPHI)
    return (jnp.cos(angles), jnp.sin(angles))


def pick_kind(per_kind, tile_kinds):
    kinds = jnp.arange(per_kind.shape[1], dtype=jnp.int32)
    chosen = tile_kinds[:, None, None] == kinds[None, :, None]
    return jnp.sum(jnp.where(chosen, per_kind, 0.0), axis=1)


def smooth(pixels, smoother_blocks, tile_slots, tile_kinds):
    tile_rows = pixels.reshape(-1, TILE)
    rows = jnp.arange(tile_rows.shape[0], dtype=jnp.int32)
    placed = (rows[:, None] == tile_slots[None, :]).astype(jnp.float32)
    picked = jnp.dot(placed.T, tile_rows, precision=lax.Precision.HIGHEST)
    inner_all = jnp.einsum("kij,tj->tki", smoother_blocks, picked, precision=precise)
    inner_part = pick_kind(inner_all, tile_kinds)
    outer_all = jnp.einsum("kji,tj->tki", smoother_blocks, inner_part, precision=precise)
    outer_part = pick_kind(outer_all, tile_kinds)
    spread = jnp.dot(placed, outer_part, precision=lax.Precision.HIGHEST)
    return spread.reshape(pixels.shape)


def per_device(
    solution,
    residual,
    direction,
    prior_inverse,
    preconditioner,
    beam_window,
    legendre,
    mode_orders,
    noise_weight,
    smoother_blocks,
    tile_slots,
    tile_kinds,
):
    nblk = lax.axis_size("blk")
    nband = lax.axis_size("band")
    band = lax.axis_index("band")
    orders_dev, parts, width = direction.shape
    cycles_all = legendre.shape[1]
    cycles_dev = cycles_all // nblk
    order_count = mode_orders.shape[0]
    norm_scale = 1.0 / math.sqrt(order_count)

    beam_here = lax.all_to_all(
        beam_window.reshape(nband, width), "band", split_axis=0, concat_axis=0, tiled=True
    )
    legendre_here = lax.dynamic_slice_in_dim(legendre, band * width, width, 2)

    weighted = (beam_here[None, :, None, :] * direction[:, None, :, :]).astype(jnp.bfloat16)
    weighted = weighted.reshape(orders_dev, nband * parts, width)
    partial = jnp.einsum(
        "sql,srl->sqr", weighted, legendre_here, preferred_element_type=jnp.float32
    )
    partial = partial.reshape(orders_dev, nband, parts, nblk, cycles_dev)
    chunk = orders_dev * parts * cycles_dev
    outgoing = partial.transpose(3, 1, 0, 2, 4).reshape(nblk * nband, chunk)
    incoming = lax.all_to_all(outgoing, EVERY, split_axis=0, concat_axis=0, tiled=True)
    cycle_coefficients = jnp.sum(
        incoming.reshape(nblk, nband, orders_dev, parts, cycles_dev), axis=1
    ).reshape(order_count, parts, cycles_dev)

    cycle_count = cycles_dev
    outer_cos, outer_sin = phases(mode_orders, NPHI // 128, 128)
    inner_cos, inner_sin = phases(mode_orders, 128, 1)
    real_part = cycle_coefficients[:, 0, :, None]
    imag_part = cycle_coefficients[:, 1, :, None]
    upper_part = real_part * outer_cos[:, None, :] - imag_part * outer_sin[:, None, :]
    lower_part = real_part * outer_sin[:, None, :] + imag_part * outer_cos[:, None, :]
    pixel_grid = jnp.einsum("mra,mb->rab", upper_part, inner_cos, precision=precise) - jnp.einsum(
        "mra,mb->rab", lower_part, inner_sin, precision=precise
    )
    pixels = norm_scale * pixel_grid.reshape(cycle_count, NPHI)
    noisy = noise_weight[0] * pixels + smooth(pixels, smoother_blocks, tile_slots, tile_kinds)
    noisy_grid = noisy.reshape(cycle_count, NPHI // 128, 128)
    cos_sums = jnp.einsum("rab,mb->mra", noisy_grid, inner_cos, precision=precise)
    sin_sums = jnp.einsum("rab,mb->mra", noisy_grid, inner_sin, precision=precise)
    real_terms = norm_scale * (
        jnp.einsum("mra,ma->mr", cos_sums, outer_cos, precision=precise)
        - jnp.einsum("mra,ma->mr", sin_sums, outer_sin, precision=precise)
    )
    imag_terms = -norm_scale * (
        jnp.einsum("mra,ma->mr", cos_sums, outer_sin, precision=precise)
        + jnp.einsum("mra,ma->mr", sin_sums, outer_cos, precision=precise)
    )
    cycle_terms = jnp.stack([real_terms, imag_terms], axis=1).astype(jnp.bfloat16)

    per_owner = cycle_terms.reshape(nblk, 1, chunk)
    returning = jnp.broadcast_to(per_owner, (nblk, nband, chunk)).reshape(nblk * nband, chunk)
    arrived = lax.all_to_all(returning, EVERY, split_axis=0, concat_axis=0, tiled=True)
    mode_terms = arrived.reshape(nblk, nband, orders_dev, parts, cycles_dev)
    mode_terms = mode_terms.transpose(2, 1, 3, 0, 4).reshape(orders_dev, nband * parts, cycles_all)
    harmonic = jnp.einsum(
        "sqr,srl->sql", mode_terms, legendre_here, preferred_element_type=jnp.float32
    ).reshape(orders_dev, nband, parts, width)
    summed = jnp.sum(beam_here[None, :, None, :] * harmonic, axis=1)

    image = prior_inverse[None, None, :] * direction + summed
    scaled_res = preconditioner[None, None, :] * residual
    scaled_image = preconditioner[None, None, :] * image
    products = jnp.stack(
        [residual * scaled_res, direction * image, scaled_res * image, scaled_image * image]
    )
    local_sums = jnp.sum(products.reshape(products.shape[0], -1), axis=1)
    shared = jnp.broadcast_to(local_sums[None], (nblk * nband, local_sums.shape[0]))
    arrived_sums = lax.all_to_all(shared, EVERY, split_axis=0, concat_axis=0, tiled=True)
    totals = lax.optimization_barrier(
        jnp.broadcast_to(
            jnp.sum(arrived_sums, axis=0)[:, None, None, None], (local_sums.shape[0], 1, 1, width)
        )
    )
    norm_now = totals[0]
    step_size = norm_now / totals[1]
    norm_next = norm_now - step_size * (2.0 * totals[2] - step_size * totals[3])
    residual_next = residual - step_size * image
    precond_next = preconditioner[None, None, :] * residual_next
    solution_next = solution + step_size * direction
    direction_next = precond_next + norm_next / norm_now * direction
    return (solution_next, residual_next, direction_next)


def solution(mesh):
    return jax.shard_map(
        per_device,
        mesh=mesh,
        in_specs=(
            P("blk", None, "band"),
            P("blk", None, "band"),
            P("blk", None, "band"),
            P("band"),
            P("band"),
            P("band", None),
            P("blk", None, None),
            P(),
            P("band", "blk", None),
            P(),
            P("blk"),
            P("blk"),
        ),
        out_specs=(P("blk", None, "band"), P("blk", None, "band"), P("blk", None, "band")),
        check_vma=False,
    )
```

```python
import math

import jax
import jax.numpy as jnp
from jax import lax
from jax.sharding import PartitionSpec as P

NPHI = 8192
TILE = 64


precise = lax.Precision.HIGH
EVERY = ("blk", "band")


def phases(mode_orders, column_count, stride):
    columns = jnp.arange(column_count, dtype=jnp.int32) * stride
    turn_counts = mode_orders[:, None] * columns[None, :] % NPHI
    angles = turn_counts.astype(jnp.float32) * (2.0 * math.pi / NPHI)
    return (jnp.cos(angles), jnp.sin(angles))


def pick_kind(per_kind, tile_kinds):
    kinds = jnp.arange(per_kind.shape[1], dtype=jnp.int32)
    chosen = tile_kinds[:, None, None] == kinds[None, :, None]
    return jnp.sum(jnp.where(chosen, per_kind, 0.0), axis=1)


def smooth(pixels, smoother_blocks, tile_slots, tile_kinds):
    tile_rows = pixels.reshape(-1, TILE)
    picked = tile_rows[tile_slots]
    inner_all = jnp.einsum("kij,tj->tki", smoother_blocks, picked, precision=precise)
    inner_part = pick_kind(inner_all, tile_kinds)
    outer_all = jnp.einsum("kji,tj->tki", smoother_blocks, inner_part, precision=precise)
    outer_part = pick_kind(outer_all, tile_kinds)
    rows = jnp.arange(tile_rows.shape[0], dtype=jnp.int32)
    placed = (rows[:, None] == tile_slots[None, :]).astype(jnp.float32)
    spread = jnp.dot(placed, outer_part, precision=lax.Precision.HIGHEST)
    return spread.reshape(pixels.shape)


def per_device(
    solution,
    residual,
    direction,
    prior_inverse,
    preconditioner,
    beam_window,
    legendre,
    mode_orders,
    noise_weight,
    smoother_blocks,
    tile_slots,
    tile_kinds,
):
    nblk = lax.axis_size("blk")
    nband = lax.axis_size("band")
    band = lax.axis_index("band")
    orders_dev, parts, width = direction.shape
    cycles_all = legendre.shape[1]
    cycles_dev = cycles_all // nblk
    order_count = mode_orders.shape[0]
    norm_scale = 1.0 / math.sqrt(order_count)

    beam_here = lax.all_to_all(
        beam_window.reshape(nband, width), "band", split_axis=0, concat_axis=0, tiled=True
    )
    legendre_here = lax.dynamic_slice_in_dim(legendre, band * width, width, 2)

    weighted = (beam_here[None, :, None, :] * direction[:, None, :, :]).astype(jnp.bfloat16)
    weighted = weighted.reshape(orders_dev, nband * parts, width)
    partial = jnp.einsum(
        "sql,srl->sqr", weighted, legendre_here, preferred_element_type=jnp.float32
    )
    partial = partial.reshape(orders_dev, nband, parts, nblk, cycles_dev)
    chunk = orders_dev * parts * cycles_dev
    outgoing = partial.transpose(3, 1, 0, 2, 4).reshape(nblk * nband, chunk)
    incoming = lax.all_to_all(outgoing, EVERY, split_axis=0, concat_axis=0, tiled=True)
    cycle_coefficients = jnp.sum(
        incoming.reshape(nblk, nband, orders_dev, parts, cycles_dev), axis=1
    ).reshape(order_count, parts, cycles_dev)

    cycle_count = cycles_dev
    outer_cos, outer_sin = phases(mode_orders, NPHI // 128, 128)
    inner_cos, inner_sin = phases(mode_orders, 128, 1)
    real_part = cycle_coefficients[:, 0, :, None]
    imag_part = cycle_coefficients[:, 1, :, None]
    upper_part = real_part * outer_cos[:, None, :] - imag_part * outer_sin[:, None, :]
    lower_part = real_part * outer_sin[:, None, :] + imag_part * outer_cos[:, None, :]
    pixel_grid = jnp.einsum("mra,mb->rab", upper_part, inner_cos, precision=precise) - jnp.einsum(
        "mra,mb->rab", lower_part, inner_sin, precision=precise
    )
    pixels = norm_scale * pixel_grid.reshape(cycle_count, NPHI)
    noisy = noise_weight[0] * pixels + smooth(pixels, smoother_blocks, tile_slots, tile_kinds)
    noisy_grid = noisy.reshape(cycle_count, NPHI // 128, 128)
    cos_sums = jnp.einsum("rab,mb->mra", noisy_grid, inner_cos, precision=precise)
    sin_sums = jnp.einsum("rab,mb->mra", noisy_grid, inner_sin, precision=precise)
    real_terms = norm_scale * (
        jnp.einsum("mra,ma->mr", cos_sums, outer_cos, precision=precise)
        - jnp.einsum("mra,ma->mr", sin_sums, outer_sin, precision=precise)
    )
    imag_terms = -norm_scale * (
        jnp.einsum("mra,ma->mr", cos_sums, outer_sin, precision=precise)
        + jnp.einsum("mra,ma->mr", sin_sums, outer_cos, precision=precise)
    )
    cycle_terms = jnp.stack([real_terms, imag_terms], axis=1).astype(jnp.bfloat16)

    per_owner = cycle_terms.reshape(nblk, 1, chunk)
    returning = jnp.broadcast_to(per_owner, (nblk, nband, chunk)).reshape(nblk * nband, chunk)
    arrived = lax.all_to_all(returning, EVERY, split_axis=0, concat_axis=0, tiled=True)
    mode_terms = arrived.reshape(nblk, nband, orders_dev, parts, cycles_dev)
    harmonic = jnp.einsum(
        "kbscj,skjl->sbcl",
        mode_terms,
        legendre_here.reshape(orders_dev, nblk, cycles_dev, width),
        preferred_element_type=jnp.float32,
    )
    summed = jnp.sum(beam_here[None, :, None, :] * harmonic, axis=1)

    image = prior_inverse[None, None, :] * direction + summed
    scaled_res = preconditioner[None, None, :] * residual
    scaled_image = preconditioner[None, None, :] * image
    products = jnp.stack(
        [residual * scaled_res, direction * image, scaled_res * image, scaled_image * image]
    )
    local_sums = jnp.sum(products.reshape(products.shape[0], -1), axis=1)
    shared = jnp.broadcast_to(local_sums[None], (nblk * nband, local_sums.shape[0]))
    arrived_sums = lax.all_to_all(shared, EVERY, split_axis=0, concat_axis=0, tiled=True)
    totals = lax.optimization_barrier(
        jnp.broadcast_to(
            jnp.sum(arrived_sums, axis=0)[:, None, None, None], (local_sums.shape[0], 1, 1, width)
        )
    )
    norm_now = totals[0]
    step_size = norm_now / totals[1]
    norm_next = norm_now - step_size * (2.0 * totals[2] - step_size * totals[3])
    residual_next = residual - step_size * image
    precond_next = preconditioner[None, None, :] * residual_next
    solution_next = solution + step_size * direction
    direction_next = precond_next + norm_next / norm_now * direction
    return (solution_next, residual_next, direction_next)


def solution(mesh):
    return jax.shard_map(
        per_device,
        mesh=mesh,
        in_specs=(
            P("blk", None, "band"),
            P("blk", None, "band"),
            P("blk", None, "band"),
            P("band"),
            P("band"),
            P("band", None),
            P("blk", None, None),
            P(),
            P("band", "blk", None),
            P(),
            P("blk"),
            P("blk"),
        ),
        out_specs=(P("blk", None, "band"), P("blk", None, "band"), P("blk", None, "band")),
        check_vma=False,
    )
```

```python
import math

import jax
import jax.numpy as jnp
from jax import lax
from jax.sharding import PartitionSpec as P

NPHI = 8192
TILE = 64


precise = lax.Precision.HIGH
EVERY = ("blk", "band")


def phases(mode_orders, column_count, stride):
    columns = jnp.arange(column_count, dtype=jnp.int32) * stride
    turn_counts = mode_orders[:, None] * columns[None, :] % NPHI
    angles = turn_counts.astype(jnp.float32) * (2.0 * math.pi / NPHI)
    return (jnp.cos(angles), jnp.sin(angles))


def pick_kind(per_kind, tile_kinds):
    kinds = jnp.arange(per_kind.shape[1], dtype=jnp.int32)
    chosen = tile_kinds[:, None, None] == kinds[None, :, None]
    return jnp.sum(jnp.where(chosen, per_kind, 0.0), axis=1)


def smooth(pixels, smoother_blocks, tile_slots, tile_kinds):
    tile_rows = pixels.reshape(-1, TILE)
    picked = tile_rows[tile_slots]
    inner_all = jnp.einsum("kij,tj->tki", smoother_blocks, picked, precision=precise)
    inner_part = pick_kind(inner_all, tile_kinds)
    outer_all = jnp.einsum("kji,tj->tki", smoother_blocks, inner_part, precision=precise)
    outer_part = pick_kind(outer_all, tile_kinds)
    rows = jnp.arange(tile_rows.shape[0], dtype=jnp.int32)
    placed = (rows[:, None] == tile_slots[None, :]).astype(jnp.float32)
    spread = jnp.dot(placed, outer_part, precision=lax.Precision.HIGHEST)
    return spread.reshape(pixels.shape)


def per_device(
    solution,
    residual,
    direction,
    prior_inverse,
    preconditioner,
    beam_window,
    legendre,
    mode_orders,
    noise_weight,
    smoother_blocks,
    tile_slots,
    tile_kinds,
):
    nblk = lax.axis_size("blk")
    nband = lax.axis_size("band")
    band = lax.axis_index("band")
    orders_dev, parts, width = direction.shape
    cycles_all = legendre.shape[1]
    cycles_dev = cycles_all // nblk
    order_count = mode_orders.shape[0]
    norm_scale = 1.0 / math.sqrt(order_count)

    beam_here = lax.all_to_all(
        beam_window.reshape(nband, width), "band", split_axis=0, concat_axis=0, tiled=True
    )
    legendre_here = lax.dynamic_slice_in_dim(legendre, band * width, width, 2)

    weighted = (beam_here[None, :, None, :] * direction[:, None, :, :]).astype(jnp.bfloat16)
    weighted = weighted.reshape(orders_dev, nband * parts, width)
    partial = jnp.einsum(
        "sql,srl->sqr", weighted, legendre_here, preferred_element_type=jnp.float32
    )
    partial = partial.reshape(orders_dev, nband, parts, nblk, cycles_dev)
    chunk = orders_dev * parts * cycles_dev
    outgoing = partial.transpose(3, 1, 0, 2, 4).reshape(nblk * nband, chunk)
    incoming = lax.all_to_all(outgoing, EVERY, split_axis=0, concat_axis=0, tiled=True)
    cycle_coefficients = jnp.sum(incoming.reshape(nblk, nband, chunk), axis=1).reshape(
        order_count, parts, cycles_dev
    )

    cycle_count = cycles_dev
    outer_cos, outer_sin = phases(mode_orders, NPHI // 128, 128)
    inner_cos, inner_sin = phases(mode_orders, 128, 1)
    real_part = cycle_coefficients[:, 0, :, None]
    imag_part = cycle_coefficients[:, 1, :, None]
    upper_part = real_part * outer_cos[:, None, :] - imag_part * outer_sin[:, None, :]
    lower_part = real_part * outer_sin[:, None, :] + imag_part * outer_cos[:, None, :]
    pixel_grid = jnp.einsum("mra,mb->rab", upper_part, inner_cos, precision=precise) - jnp.einsum(
        "mra,mb->rab", lower_part, inner_sin, precision=precise
    )
    pixels = norm_scale * pixel_grid.reshape(cycle_count, NPHI)
    noisy = noise_weight[0] * pixels + smooth(pixels, smoother_blocks, tile_slots, tile_kinds)
    noisy_grid = noisy.reshape(cycle_count, NPHI // 128, 128)
    cos_sums = jnp.einsum("rab,mb->mra", noisy_grid, inner_cos, precision=precise)
    sin_sums = jnp.einsum("rab,mb->mra", noisy_grid, inner_sin, precision=precise)
    real_terms = norm_scale * (
        jnp.einsum("mra,ma->mr", cos_sums, outer_cos, precision=precise)
        - jnp.einsum("mra,ma->mr", sin_sums, outer_sin, precision=precise)
    )
    imag_terms = -norm_scale * (
        jnp.einsum("mra,ma->mr", cos_sums, outer_sin, precision=precise)
        + jnp.einsum("mra,ma->mr", sin_sums, outer_cos, precision=precise)
    )
    cycle_terms = jnp.stack([real_terms, imag_terms], axis=1).astype(jnp.bfloat16)

    per_owner = cycle_terms.reshape(nblk, 1, chunk)
    returning = jnp.broadcast_to(per_owner, (nblk, nband, chunk)).reshape(nblk * nband, chunk)
    arrived = lax.all_to_all(returning, EVERY, split_axis=0, concat_axis=0, tiled=True)
    mode_terms = arrived.reshape(nblk, nband, orders_dev, parts, cycles_dev)
    mode_terms = mode_terms.transpose(2, 1, 3, 0, 4).reshape(orders_dev, nband * parts, cycles_all)
    harmonic = jnp.einsum(
        "sqr,srl->sql", mode_terms, legendre_here, preferred_element_type=jnp.float32
    ).reshape(orders_dev, nband, parts, width)
    summed = jnp.sum(beam_here[None, :, None, :] * harmonic, axis=1)

    image = prior_inverse[None, None, :] * direction + summed
    scaled_res = preconditioner[None, None, :] * residual
    scaled_image = preconditioner[None, None, :] * image
    products = jnp.stack(
        [residual * scaled_res, direction * image, scaled_res * image, scaled_image * image]
    )
    local_sums = jnp.sum(products.reshape(products.shape[0], -1), axis=1)
    shared = jnp.broadcast_to(local_sums[None], (nblk * nband, local_sums.shape[0]))
    arrived_sums = lax.all_to_all(shared, EVERY, split_axis=0, concat_axis=0, tiled=True)
    totals = lax.optimization_barrier(
        jnp.broadcast_to(
            jnp.sum(arrived_sums, axis=0)[:, None, None, None], (local_sums.shape[0], 1, 1, width)
        )
    )
    norm_now = totals[0]
    step_size = norm_now / totals[1]
    norm_next = norm_now - step_size * (2.0 * totals[2] - step_size * totals[3])
    residual_next = residual - step_size * image
    precond_next = preconditioner[None, None, :] * residual_next
    solution_next = solution + step_size * direction
    direction_next = precond_next + norm_next / norm_now * direction
    return (solution_next, residual_next, direction_next)


def solution(mesh):
    return jax.shard_map(
        per_device,
        mesh=mesh,
        in_specs=(
            P("blk", None, "band"),
            P("blk", None, "band"),
            P("blk", None, "band"),
            P("band"),
            P("band"),
            P("band", None),
            P("blk", None, None),
            P(),
            P("band", "blk", None),
            P(),
            P("blk"),
            P("blk"),
        ),
        out_specs=(P("blk", None, "band"), P("blk", None, "band"), P("blk", None, "band")),
        check_vma=False,
    )
```

```python
import math

import jax
import jax.numpy as jnp
from jax import lax
from jax.sharding import PartitionSpec as P

NPHI = 8192
TILE = 64


precise = lax.Precision.HIGH
EVERY = ("blk", "band")


def phases(mode_orders, column_count, stride):
    columns = jnp.arange(column_count, dtype=jnp.int32) * stride
    turn_counts = mode_orders[:, None] * columns[None, :] % NPHI
    angles = turn_counts.astype(jnp.float32) * (2.0 * math.pi / NPHI)
    return (jnp.cos(angles), jnp.sin(angles))


def pick_kind(per_kind, tile_kinds):
    kinds = jnp.arange(per_kind.shape[1], dtype=jnp.int32)
    chosen = tile_kinds[:, None, None] == kinds[None, :, None]
    return jnp.sum(jnp.where(chosen, per_kind, 0.0), axis=1)


def smooth(pixels, smoother_blocks, tile_slots, tile_kinds):
    tile_rows = pixels.reshape(-1, TILE)
    picked = tile_rows[tile_slots]
    inner_all = jnp.einsum("kij,tj->tki", smoother_blocks, picked, precision=precise)
    inner_part = pick_kind(inner_all, tile_kinds)
    outer_all = jnp.einsum("kji,tj->tki", smoother_blocks, inner_part, precision=precise)
    outer_part = pick_kind(outer_all, tile_kinds)
    rows = jnp.arange(tile_rows.shape[0], dtype=jnp.int32)
    placed = (rows[:, None] == tile_slots[None, :]).astype(jnp.float32)
    spread = jnp.dot(placed, outer_part, precision=lax.Precision.HIGHEST)
    return spread.reshape(pixels.shape)


def per_device(
    solution,
    residual,
    direction,
    prior_inverse,
    preconditioner,
    beam_window,
    legendre,
    mode_orders,
    noise_weight,
    smoother_blocks,
    tile_slots,
    tile_kinds,
):
    nblk = lax.axis_size("blk")
    nband = lax.axis_size("band")
    band = lax.axis_index("band")
    orders_dev, parts, width = direction.shape
    cycles_all = legendre.shape[1]
    cycles_dev = cycles_all // nblk
    order_count = mode_orders.shape[0]
    norm_scale = 1.0 / math.sqrt(order_count)

    beam_here = lax.all_to_all(
        beam_window.reshape(nband, width), "band", split_axis=0, concat_axis=0, tiled=True
    )
    legendre_here = lax.dynamic_slice_in_dim(legendre, band * width, width, 2)

    weighted = (beam_here[None, :, None, :] * direction[:, None, :, :]).astype(jnp.bfloat16)
    weighted = weighted.reshape(orders_dev, nband * parts, width)
    partial = jnp.einsum(
        "sql,srl->sqr", weighted, legendre_here, preferred_element_type=jnp.float32
    )
    partial = partial.reshape(orders_dev, nband, parts, nblk, cycles_dev)
    chunk = orders_dev * parts * cycles_dev
    outgoing = partial.transpose(3, 1, 0, 2, 4).reshape(nblk * nband, chunk)
    incoming = lax.all_to_all(outgoing, EVERY, split_axis=0, concat_axis=0, tiled=True)
    cycle_coefficients = jnp.sum(
        incoming.reshape(nblk, nband, orders_dev, parts, cycles_dev), axis=1
    ).reshape(order_count, parts, cycles_dev)

    cycle_count = cycles_dev
    outer_cos, outer_sin = phases(mode_orders, NPHI // 128, 128)
    inner_cos, inner_sin = phases(mode_orders, 128, 1)
    real_part = cycle_coefficients[:, 0, :, None]
    imag_part = cycle_coefficients[:, 1, :, None]
    upper_part = real_part * outer_cos[:, None, :] - imag_part * outer_sin[:, None, :]
    lower_part = real_part * outer_sin[:, None, :] + imag_part * outer_cos[:, None, :]
    pixel_grid = jnp.einsum("mra,mb->rab", upper_part, inner_cos, precision=precise) - jnp.einsum(
        "mra,mb->rab", lower_part, inner_sin, precision=precise
    )
    pixels = norm_scale * pixel_grid.reshape(cycle_count, NPHI)
    noisy = noise_weight[0] * pixels + smooth(pixels, smoother_blocks, tile_slots, tile_kinds)
    noisy_grid = noisy.reshape(cycle_count, NPHI // 128, 128)
    cos_sums = jnp.einsum("rab,mb->mra", noisy_grid, inner_cos, precision=precise)
    sin_sums = jnp.einsum("rab,mb->mra", noisy_grid, inner_sin, precision=precise)
    oc, os_ = outer_cos[:, None, :], outer_sin[:, None, :]
    both_terms = jnp.stack(
        [cos_sums * oc - sin_sums * os_, -(cos_sums * os_ + sin_sums * oc)], axis=1
    )
    cycle_terms = (norm_scale * jnp.sum(both_terms, axis=3)).astype(jnp.bfloat16)

    per_owner = cycle_terms.reshape(nblk, 1, chunk)
    returning = jnp.broadcast_to(per_owner, (nblk, nband, chunk)).reshape(nblk * nband, chunk)
    arrived = lax.all_to_all(returning, EVERY, split_axis=0, concat_axis=0, tiled=True)
    mode_terms = arrived.reshape(nblk, nband, orders_dev, parts, cycles_dev)
    mode_terms = mode_terms.transpose(2, 1, 3, 0, 4).reshape(orders_dev, nband * parts, cycles_all)
    harmonic = jnp.einsum(
        "sqr,srl->sql", mode_terms, legendre_here, preferred_element_type=jnp.float32
    ).reshape(orders_dev, nband, parts, width)
    summed = jnp.sum(beam_here[None, :, None, :] * harmonic, axis=1)

    image = prior_inverse[None, None, :] * direction + summed
    scaled_res = preconditioner[None, None, :] * residual
    scaled_image = preconditioner[None, None, :] * image
    products = jnp.stack(
        [residual * scaled_res, direction * image, scaled_res * image, scaled_image * image]
    )
    local_sums = jnp.sum(products.reshape(products.shape[0], -1), axis=1)
    shared = jnp.broadcast_to(local_sums[None], (nblk * nband, local_sums.shape[0]))
    arrived_sums = lax.all_to_all(shared, EVERY, split_axis=0, concat_axis=0, tiled=True)
    totals = lax.optimization_barrier(
        jnp.broadcast_to(
            jnp.sum(arrived_sums, axis=0)[:, None, None, None], (local_sums.shape[0], 1, 1, width)
        )
    )
    norm_now = totals[0]
    step_size = norm_now / totals[1]
    norm_next = norm_now - step_size * (2.0 * totals[2] - step_size * totals[3])
    residual_next = residual - step_size * image
    precond_next = preconditioner[None, None, :] * residual_next
    solution_next = solution + step_size * direction
    direction_next = precond_next + norm_next / norm_now * direction
    return (solution_next, residual_next, direction_next)


def solution(mesh):
    return jax.shard_map(
        per_device,
        mesh=mesh,
        in_specs=(
            P("blk", None, "band"),
            P("blk", None, "band"),
            P("blk", None, "band"),
            P("band"),
            P("band"),
            P("band", None),
            P("blk", None, None),
            P(),
            P("band", "blk", None),
            P(),
            P("blk"),
            P("blk"),
        ),
        out_specs=(P("blk", None, "band"), P("blk", None, "band"), P("blk", None, "band")),
        check_vma=False,
    )
```
